256 devices in a mesh: tile: 64 (over y, z, core), sub: 4 (over x).
Axes of the slice: x: 4, y: 4, z: 8, core: 2. Of those that a mesh axis runs over, the one named last changes fastest.
Arguments:
- atm_fields: float32 [6, 2048, 128], P(None, ('tile', 'sub')), may hold values from -6 to 6
- pair_atm: int32 [5120], P(('tile', 'sub')), may hold values from 0 to 7
- pair_land: int32 [5120], P(('tile', 'sub')), may hold values from 0 to 4095, as said below
- pair_weight: bfloat16 [5120, 3, 128, 512], P(('tile', 'sub')), may hold values from -0.3125 to 0.3125
- land_mask: int32 [2097152], P(('tile', 'sub')), may hold values 0 or 1
- conductance: float32 [20, 2097152], P(None, ('tile', 'sub')), may hold values from 0.1 to 3
- soil_moisture: float32 [20, 2097152], P(None, ('tile', 'sub')), may hold values from 0.1 to 0.5
- river_owner: int32 [16384], P(('tile', 'sub')), may hold values from 0 to 63, as said below
Outputs:
- land_forcing: bfloat16 [6, 2097152], P(None, ('tile', 'sub'))
- soil_state: float32 [20, 2097152], P(None, ('tile', 'sub'))
- river_runoff: float32 [64, 4, 64, 2, 128], P('tile', 'sub')
- river_blocks: int32 [64, 4, 64, 2], P('tile', 'sub')
The draws below stay inside these ranges and needn't reach their ends.
Inputs may be any that keep to these rules, and one draw needn't show every extreme that they name: `pair_land`: the land block of a pair lies in the tile of the pair's atmosphere device or in one of the two tiles beside it, cyclically over the 64 tiles (device d = t * 4 + s owns land blocks d * 16 onward). At most 4 pairs of one device name land blocks of one device, and in every tile some land device receives exactly 4 pairs from each of the tile's 4 devices. `river_owner`: A block goes to the river owner device on the given tile with the same sub index. At most 2 blocks of one device go to one owner, and for every sub index some owner receives exactly 2 blocks from each device of that sub index.
All inputs are finite; a program needn't handle non-finite values. No bound on the sum of `land_mask` on one device may be relied on, other than what follows from the above.
Results may differ from the reference program's by a relative error of at most 0.0049.
Values sent between devices are 32-bit elements; how exact they have to be, the bound alone decides.
No kernel may reach another device: no remote copies, remote signals or barrier semaphores. Data moves between devices by JAX's collectives and lax.ppermute only.
A program may use at most 64 MiB of HBM per device.

```python
import math
import jax
import jax.numpy as jnp
from jax import lax

F = 6
SOIL = 20
SOIL_STEPS = 4
AX = 128
LBLK = 512
RBLK = 128
CAP_P = 4
AROWS = 8
PAIRS_DEV = 20
LB_DEV = 16
RB_DEV = 64
CAP_R = 2
ATM_ROWS = 2048
PAIRS = 5120
LAND_BLOCKS = 4096
LAND = 2097152
N_TILE = 64
N_SUB = 4


def spread_slots(key, row_count, group_count, capacity, count, forced):
    first_key, second_key = jax.random.split(key)
    slot_total = group_count * capacity
    orders = jax.vmap(lambda k: jax.random.permutation(k, slot_total))(jax.random.split(first_key, row_count))
    orders = orders.astype(jnp.int32)
    inside = (orders // capacity == forced[:, None]).astype(jnp.int32)
    placing = jnp.argsort(inside, axis=1, stable=True)
    others = jnp.take_along_axis(orders, placing, axis=1)[:, :count - capacity]
    fixed_part = forced[:, None] * capacity + jnp.arange(capacity, dtype=jnp.int32)[None, :]
    chosen = jnp.concatenate([fixed_part, others], axis=1)
    shuffle = jax.vmap(lambda k: jax.random.permutation(k, count))(jax.random.split(second_key, row_count))
    chosen = jnp.take_along_axis(chosen, shuffle.astype(jnp.int32), axis=1)
    return chosen // capacity


def draw_pair_land(key, part):
    devices = N_TILE * N_SUB
    first_key, second_key, third_key = jax.random.split(jax.random.fold_in(key, 11), 3)
    forced_tile = jax.random.randint(first_key, (N_TILE,), 0, 3 * N_SUB, dtype=jnp.int32)
    forced = jnp.repeat(forced_tile, N_SUB)
    group_id = spread_slots(second_key, devices, 3 * N_SUB, CAP_P, PAIRS_DEV, forced)
    local_block = jax.random.randint(third_key, (devices, PAIRS_DEV), 0, LB_DEV, dtype=jnp.int32)
    tile_index = (jnp.arange(devices, dtype=jnp.int32) // N_SUB)[:, None]
    dest_tile = (tile_index + group_id // N_SUB - 1 + N_TILE) % N_TILE
    land_block = (dest_tile * N_SUB + group_id % N_SUB) * LB_DEV + local_block
    return land_block.reshape(-1).astype(jnp.int32)


def draw_river_owner(key, part):
    devices = N_TILE * N_SUB
    first_key, second_key = jax.random.split(jax.random.fold_in(key, 23))
    forced_sub = jax.random.randint(first_key, (N_SUB,), 0, N_TILE, dtype=jnp.int32)
    forced = jnp.tile(forced_sub, N_TILE)
    owners = spread_slots(second_key, devices, N_TILE, CAP_R, RB_DEV, forced)
    return owners.reshape(-1).astype(jnp.int32)


def with_ends(drawn, stream_key, smallest, high):
    index_at = [jax.random.randint(jax.random.fold_in(stream_key, axis), (), 0, length) for axis, length in enumerate(drawn.shape)]
    main_axis = drawn.shape.index(max(drawn.shape))
    beside = index_at[:main_axis] + [(index_at[main_axis] + 1) % drawn.shape[main_axis]] + index_at[main_axis + 1:]
    return drawn.at[tuple(index_at)].set(smallest).at[tuple(beside)].set(high)


def shard_levels(own_key, shape, shards, least, largest):
    def one(dim, shards_of):
        draws = jax.random.uniform(jax.random.fold_in(jax.random.fold_in(own_key, 6), dim), (shards_of,), jnp.float32, least / len(shards), largest / len(shards))
        return jnp.repeat(jnp.exp(draws), shape[dim] // shards_of).reshape((-1,) + (1,) * (len(shape) - dim - 1))

    loudness = one(*shards[0])
    for cut in shards[1:]:
        loudness = loudness * one(*cut)
    return loudness


def centred(rng, shape, width, bound, cuts=(), kind=jnp.bfloat16):
    result = jax.random.normal(rng, shape, jnp.float32) * width
    if len(cuts) > 0:
        result = shard_levels(rng, shape, cuts, -0.22, 0.18) * result
    return jnp.clip(result, min=-bound, max=bound).astype(kind)


def setup_inputs(seed: int = 0) -> dict:
    streams_of = jax.random.split(jax.random.key(seed), 9)
    atm_fields = centred(streams_of[0], (F, ATM_ROWS, AX), 1.0, 6.0, ((1, 256),), jnp.float32)
    pair_atm = with_ends(jax.random.randint(streams_of[1], (PAIRS,), 0, AROWS), jax.random.fold_in(streams_of[1], 1), 0, AROWS - 1).astype(jnp.int32)
    pair_land = draw_pair_land(jax.random.fold_in(streams_of[8], 71), 0)
    pair_weight = centred(streams_of[3], (PAIRS, 3, AX, LBLK), (3 * AX) ** -0.5, 0.3125, ((0, 256),))
    land_mask = with_ends((jax.random.randint(streams_of[4], (LAND,), 0, 10) < 7).astype(jnp.int32), jax.random.fold_in(streams_of[4], 1), 0, 1)
    conductance = jnp.clip(jnp.exp(math.log(3.0) - 3.4011974 * jax.random.uniform(streams_of[5], (SOIL, LAND), jnp.float32) ** shard_levels(streams_of[5], (SOIL, LAND), ((1, 256),), -0.2, 0.2)), 0.1, 3.0)
    soil_moisture = jnp.clip(0.1 + 0.4 * jax.random.uniform(streams_of[6], (SOIL, LAND), jnp.float32) ** shard_levels(streams_of[6], (SOIL, LAND), ((1, 256),), -0.2, 0.2), 0.1, 0.5)
    river_owner = draw_river_owner(jax.random.fold_in(streams_of[8], 71), 0)
    return dict(atm_fields=atm_fields, pair_atm=pair_atm, pair_land=pair_land, pair_weight=pair_weight, land_mask=land_mask, conductance=conductance, soil_moisture=soil_moisture, river_owner=river_owner)


def x_gradient(fields):
    inner = (fields[:, :, 2:] - fields[:, :, :-2]) * 0.5
    first = fields[:, :, 1:2] - fields[:, :, 0:1]
    last = fields[:, :, -1:] - fields[:, :, -2:-1]
    return jnp.concatenate([first, inner, last], axis=2)


def column_factors(conductance):
    layers = conductance.shape[0]
    inverse = []
    ratios = []
    for k in range(layers):
        diagonal = 1.0 + conductance[k]
        if k > 0:
            diagonal = diagonal + conductance[k - 1] - conductance[k - 1] * conductance[k - 1] * inverse[k - 1]
        pivot_inv = 1.0 / diagonal
        inverse.append(pivot_inv)
        ratios.append(-conductance[k] * pivot_inv)
    return inverse, ratios


def column_solve(moisture, source, conductance, inverse, ratios):
    layers = len(inverse)
    forward = []
    for k in range(layers):
        if k == 0:
            column_value = moisture[0] + source
        else:
            column_value = moisture[k] + conductance[k - 1] * forward[k - 1]
        forward.append(column_value * inverse[k])
    solved = [forward[layers - 1]]
    for k in range(layers - 2, -1, -1):
        solved.insert(0, forward[k] - ratios[k] * solved[0])
    return jnp.stack(solved)


def soil_update(forcing, land_mask, conductance, soil_moisture):
    wetness = land_mask.astype(jnp.float32)
    source = wetness * (jax.nn.softplus(forcing[0]) * jax.nn.sigmoid(forcing[1])
                        - 0.5 * jax.nn.sigmoid(forcing[2]) * jax.nn.softplus(forcing[3]))
    surface = wetness * jax.nn.softplus(forcing[0]) * (1.0 - jax.nn.sigmoid(forcing[1]))
    inverse, ratios = column_factors(conductance)
    bottom = conductance.shape[0] - 1
    moisture = soil_moisture
    drainage = jnp.zeros_like(surface)
    for substep in range(SOIL_STEPS):
        moisture = column_solve(moisture, source, conductance, inverse, ratios)
        drainage = drainage + conductance[bottom] * moisture[bottom]
    runoff = wetness * (SOIL_STEPS * surface + drainage)
    return moisture, runoff


def reference(atm_fields, pair_atm, pair_land, pair_weight, land_mask, conductance, soil_moisture, river_owner):
    devices = N_TILE * N_SUB
    grad_x = x_gradient(atm_fields)
    grad_y = (jnp.roll(atm_fields, -1, 1) - jnp.roll(atm_fields, 1, 1)) * 0.5
    stacked = jnp.concatenate([atm_fields, grad_x, grad_y], axis=2).astype(jnp.bfloat16)
    stacked_dev = stacked.reshape(F, devices, AROWS, 3 * AX).transpose(1, 0, 2, 3)
    atm_dev = pair_atm.reshape(devices, PAIRS_DEV)
    weight_dev = pair_weight.reshape(devices, PAIRS_DEV, 3 * AX, LBLK)

    def one_device(inputs):
        device_rows, row_index, weights = inputs
        picked = device_rows[:, row_index, :].astype(jnp.float32)
        return jnp.einsum('fpk,pkl->pfl', picked, weights.astype(jnp.float32))

    partial_value = lax.map(one_device, (stacked_dev, atm_dev, weight_dev))
    blocks = jnp.zeros((LAND_BLOCKS, F, LBLK), jnp.float32).at[pair_land].add(partial_value.reshape(PAIRS, F, LBLK))
    forcing = blocks.transpose(1, 0, 2).reshape(F, LAND)
    land_forcing = forcing.astype(jnp.bfloat16)
    moisture, runoff = soil_update(forcing, land_mask, conductance, soil_moisture)

    runoff_blocks = runoff.reshape(devices, RB_DEV, RBLK)
    owners = river_owner.reshape(devices, RB_DEV)
    hits = (owners[:, :, None] == jnp.arange(N_TILE, dtype=jnp.int32)[None, None, :]).astype(jnp.int32)
    earlier = jnp.cumsum(hits, axis=1) - hits
    ranks = jnp.sum(earlier * hits, axis=2).astype(jnp.int32)
    slots = (owners * CAP_R + ranks).astype(jnp.int32)
    device_ids = jnp.arange(devices, dtype=jnp.int32)[:, None]
    block_ids = jnp.arange(devices * RB_DEV, dtype=jnp.int32).reshape(devices, RB_DEV)
    values = jnp.zeros((devices, N_TILE * CAP_R, RBLK), jnp.float32).at[device_ids, slots].set(runoff_blocks)
    numbers = jnp.full((devices, N_TILE * CAP_R), -1, jnp.int32).at[device_ids, slots].set(block_ids)
    river_runoff = values.reshape(N_TILE, N_SUB, N_TILE, CAP_R, RBLK).transpose(2, 1, 0, 3, 4)
    river_blocks = numbers.reshape(N_TILE, N_SUB, N_TILE, CAP_R).transpose(2, 1, 0, 3)
    return (land_forcing, moisture, river_runoff, river_blocks)
```

```python
import jax
import jax.numpy as jnp
from jax import lax
from jax.sharding import PartitionSpec as P

SOIL_STEPS = 4
LBLK = 512
RBLK = 128
LB_DEV = 16


def passed_along(block, axis, distance):
    devices = range(lax.axis_size(axis))
    route = [((i - distance) % len(devices), i) for i in devices]
    return lax.ppermute(block, axis, route)


def padded(array, sides, width):
    for axis, dim in sides:
        devices, length = (lax.axis_size(axis), array.shape[dim])
        up = [(i, (i + 1) % devices) for i in range(devices)]
        down = [(j, i) for i, j in up]
        last = lax.slice_in_dim(array, length - width, length, axis=dim)
        initial = lax.slice_in_dim(array, 0, width, axis=dim)
        before = lax.ppermute(last, axis, up)
        after = lax.ppermute(initial, axis, down)
        array = jnp.concatenate([before, array, after], axis=dim)
    return array


def x_gradient(fields):
    inner = (fields[:, :, 2:] - fields[:, :, :-2]) * 0.5
    first = fields[:, :, 1:2] - fields[:, :, 0:1]
    last = fields[:, :, -1:] - fields[:, :, -2:-1]
    return jnp.concatenate([first, inner, last], axis=2)


def column_factors(conductance):
    layers = conductance.shape[0]
    inverse = []
    ratios = []
    for k in range(layers):
        diagonal = 1.0 + conductance[k]
        if k > 0:
            diagonal = (
                diagonal
                + conductance[k - 1]
                - conductance[k - 1] * conductance[k - 1] * inverse[k - 1]
            )
        pivot_inv = 1.0 / diagonal
        inverse.append(pivot_inv)
        ratios.append(-conductance[k] * pivot_inv)
    return (inverse, ratios)


def column_solve(moisture, source, conductance, inverse, ratios):
    layers = len(inverse)
    forward = []
    for k in range(layers):
        if k == 0:
            column_value = moisture[0] + source
        else:
            column_value = moisture[k] + conductance[k - 1] * forward[k - 1]
        forward.append(column_value * inverse[k])
    solved = [forward[layers - 1]]
    for k in range(layers - 2, -1, -1):
        solved.insert(0, forward[k] - ratios[k] * solved[0])
    return jnp.stack(solved)


def soil_update(forcing, land_mask, conductance, soil_moisture):
    wetness = land_mask.astype(jnp.float32)
    source = wetness * (
        jax.nn.softplus(forcing[0]) * jax.nn.sigmoid(forcing[1])
        - 0.5 * jax.nn.sigmoid(forcing[2]) * jax.nn.softplus(forcing[3])
    )
    surface = wetness * jax.nn.softplus(forcing[0]) * (1.0 - jax.nn.sigmoid(forcing[1]))
    inverse, ratios = column_factors(conductance)
    bottom = conductance.shape[0] - 1
    moisture = soil_moisture
    drainage = jnp.zeros_like(surface)
    for substep in range(SOIL_STEPS):
        moisture = column_solve(moisture, source, conductance, inverse, ratios)
        drainage = drainage + conductance[bottom] * moisture[bottom]
    runoff = wetness * (SOIL_STEPS * surface + drainage)
    return (moisture, runoff)


CAP_P = 4
CAP_R = 2


def route_partials(flat_terms, pair_land, tile_count, sub_count, tile_index, sub_index):
    pair_count, width = flat_terms.shape
    owner_device = pair_land // LB_DEV
    tile_step = (owner_device // sub_count - tile_index + 1 + tile_count) % tile_count
    sub_step = (owner_device % sub_count - sub_index + sub_count) % sub_count
    group_count = 3 * sub_count
    group_id = tile_step * sub_count + sub_step
    hits = (group_id[:, None] == jnp.arange(group_count, dtype=jnp.int32)[None, :]).astype(jnp.int32)
    ranks = jnp.sum((jnp.cumsum(hits, axis=0) - hits) * hits, axis=1)
    slot_id = group_id * CAP_P + ranks
    slot_count = group_count * CAP_P
    placing = slot_id[None, :] == jnp.arange(slot_count, dtype=jnp.int32)[:, None]
    source = jnp.sum(jnp.where(placing, jnp.arange(pair_count, dtype=jnp.int32)[None, :] + 1, 0), axis=1) - 1
    filled = source >= 0
    picked = jnp.maximum(source, 0)
    rows = jnp.where(filled[:, None], flat_terms[picked], 0.0)
    ids = jnp.where(filled, pair_land[picked] % LB_DEV, -1).astype(jnp.float32)
    ids = jnp.pad(ids.reshape(group_count, CAP_P), ((0, 0), (0, 128 - CAP_P)))
    messages = jnp.concatenate([rows.reshape(group_count, CAP_P * width), ids], axis=1)
    devices = tile_count * sub_count
    received = []
    for tile_offset in range(3):
        for sub_offset in range(sub_count):
            message = messages[tile_offset * sub_count + sub_offset]
            if tile_offset == 1 and sub_offset == 0:
                received.append(message)
                continue
            route = []
            for d in range(devices):
                t, s = divmod(d, sub_count)
                target = ((t + tile_offset - 1) % tile_count) * sub_count + (s + sub_offset) % sub_count
                route.append((d, target))
            received.append(lax.ppermute(message, ("tile", "sub"), route))
    got = jnp.stack(received)
    data = got[:, : CAP_P * width].reshape(slot_count, width)
    got_ids = got[:, CAP_P * width : CAP_P * width + CAP_P].reshape(slot_count)
    selector = (got_ids[None, :] == jnp.arange(LB_DEV, dtype=jnp.float32)[:, None]).astype(jnp.float32)
    return jnp.dot(selector, data, precision=lax.Precision.HIGHEST)


def on_device(
    atm_fields, pair_atm, pair_land, pair_weight, land_mask, conductance, soil_moisture, river_owner
):
    tile_count = lax.axis_size("tile")
    sub_count = lax.axis_size("sub")
    tile_index = lax.axis_index("tile")
    sub_index = lax.axis_index("sub")
    field_count, row_count, row_width = atm_fields.shape
    extended = padded(atm_fields, ((("tile", "sub"), 1),), 1)
    grad_x = x_gradient(atm_fields)
    grad_y = (extended[:, 2:, :] - extended[:, :-2, :]) * 0.5
    stacked = jnp.concatenate([atm_fields, grad_x, grad_y], axis=2).astype(jnp.bfloat16)
    pair_count = pair_atm.shape[0]
    picked = stacked[:, pair_atm, :]
    weights = pair_weight.reshape(pair_count, 3 * row_width, LBLK)
    partial_value = jnp.einsum("fpk,pkl->pfl", picked, weights, preferred_element_type=jnp.float32)
    flat_terms = partial_value.reshape(pair_count, field_count * LBLK)
    owned_sums = route_partials(flat_terms, pair_land, tile_count, sub_count, tile_index, sub_index)
    forcing = owned_sums.reshape(LB_DEV, field_count, LBLK).transpose(1, 0, 2).reshape(
        field_count, LB_DEV * LBLK
    )
    land_forcing = forcing.astype(jnp.bfloat16)
    moisture, runoff = soil_update(forcing, land_mask, conductance, soil_moisture)
    block_count = runoff.shape[0] // RBLK
    capacity = CAP_R
    runoff_blocks = runoff.reshape(block_count, RBLK)
    hits = (river_owner[:, None] == jnp.arange(tile_count, dtype=jnp.int32)[None, :]).astype(
        jnp.int32
    )
    ranks = jnp.sum((jnp.cumsum(hits, axis=0) - hits) * hits, axis=1)
    slot_id = river_owner * capacity + ranks
    placing = slot_id[None, :] == jnp.arange(tile_count * capacity, dtype=jnp.int32)[:, None]
    values = jnp.dot(placing.astype(jnp.float32), runoff_blocks, precision=lax.Precision.HIGHEST)
    values = values.reshape(tile_count, capacity * RBLK)
    block_ids = (tile_index * sub_count + sub_index) * block_count + jnp.arange(
        block_count, dtype=jnp.int32
    )
    numbers = jnp.sum(jnp.where(placing, block_ids[None, :] + 1, 0), axis=1) - 1
    numbers = numbers.astype(jnp.float32).reshape(tile_count, capacity)
    numbers = jnp.pad(numbers, ((0, 0), (0, RBLK - capacity)))
    packed = jnp.concatenate([values, numbers], axis=1)
    got = lax.all_to_all(packed, "tile", split_axis=0, concat_axis=0, tiled=True)
    river_runoff = got[:, : capacity * RBLK].reshape(tile_count, capacity, RBLK)[None, None]
    river_blocks = got[:, capacity * RBLK : capacity * RBLK + capacity].astype(jnp.int32)[None, None]
    return (land_forcing, moisture, river_runoff, river_blocks)


def solution(mesh):
    return jax.shard_map(
        on_device,
        mesh=mesh,
        in_specs=(
            P(None, ("tile", "sub"), None),
            P(("tile", "sub")),
            P(("tile", "sub")),
            P(("tile", "sub"), None, None, None),
            P(("tile", "sub")),
            P(None, ("tile", "sub")),
            P(None, ("tile", "sub")),
            P(("tile", "sub")),
        ),
        out_specs=(
            P(None, ("tile", "sub")),
            P(None, ("tile", "sub")),
            P("tile", "sub", None, None, None),
            P("tile", "sub", None, None),
        ),
        check_vma=False,
    )
```

```python
import jax
import jax.numpy as jnp
from jax import lax
from jax.sharding import PartitionSpec as P
from jax.experimental import pallas as pl
from jax.experimental.pallas import tpu as pltpu

SOIL_STEPS = 4
LBLK = 512
RBLK = 128
LB_DEV = 16


def passed_along(block, axis, distance):
    devices = range(lax.axis_size(axis))
    route = [((i - distance) % len(devices), i) for i in devices]
    return lax.ppermute(block, axis, route)


def padded(array, sides, width):
    for axis, dim in sides:
        devices, length = (lax.axis_size(axis), array.shape[dim])
        up = [(i, (i + 1) % devices) for i in range(devices)]
        down = [(j, i) for i, j in up]
        last = lax.slice_in_dim(array, length - width, length, axis=dim)
        initial = lax.slice_in_dim(array, 0, width, axis=dim)
        before = lax.ppermute(last, axis, up)
        after = lax.ppermute(initial, axis, down)
        array = jnp.concatenate([before, array, after], axis=dim)
    return array


def x_gradient(fields):
    inner = (fields[:, :, 2:] - fields[:, :, :-2]) * 0.5
    first = fields[:, :, 1:2] - fields[:, :, 0:1]
    last = fields[:, :, -1:] - fields[:, :, -2:-1]
    return jnp.concatenate([first, inner, last], axis=2)


def column_factors(conductance):
    layers = conductance.shape[0]
    inverse = []
    ratios = []
    for k in range(layers):
        diagonal = 1.0 + conductance[k]
        if k > 0:
            diagonal = (
                diagonal
                + conductance[k - 1]
                - conductance[k - 1] * conductance[k - 1] * inverse[k - 1]
            )
        pivot_inv = 1.0 / diagonal
        inverse.append(pivot_inv)
        ratios.append(-conductance[k] * pivot_inv)
    return (inverse, ratios)


def column_solve(moisture, source, conductance, inverse, ratios):
    layers = len(inverse)
    forward = []
    for k in range(layers):
        if k == 0:
            column_value = moisture[0] + source
        else:
            column_value = moisture[k] + conductance[k - 1] * forward[k - 1]
        forward.append(column_value * inverse[k])
    solved = [forward[layers - 1]]
    for k in range(layers - 2, -1, -1):
        solved.insert(0, forward[k] - ratios[k] * solved[0])
    return jnp.stack(solved)


def soil_kernel(source_ref, surface_ref, wet_ref, cond_ref, moist_ref, out_ref, runoff_ref):
    layers = cond_ref.shape[0]
    groups = cond_ref.shape[1] // 8

    def one_group(g, carry):
        rows = pl.ds(pl.multiple_of(g * 8, 8), 8)
        cond = [cond_ref[k, rows, :] for k in range(layers)]
        inverse = []
        ratios = []
        for k in range(layers):
            diagonal = 1.0 + cond[k]
            if k > 0:
                diagonal = diagonal + cond[k - 1] - cond[k - 1] * cond[k - 1] * inverse[k - 1]
            pivot_inv = 1.0 / diagonal
            inverse.append(pivot_inv)
            ratios.append(-cond[k] * pivot_inv)
        source = source_ref[rows, :]
        moisture = [moist_ref[k, rows, :] for k in range(layers)]
        drainage = jnp.zeros_like(source)
        for substep in range(SOIL_STEPS):
            forward = []
            for k in range(layers):
                if k == 0:
                    column_value = moisture[0] + source
                else:
                    column_value = moisture[k] + cond[k - 1] * forward[k - 1]
                forward.append(column_value * inverse[k])
            solved = [forward[layers - 1]]
            for k in range(layers - 2, -1, -1):
                solved.insert(0, forward[k] - ratios[k] * solved[0])
            moisture = solved
            drainage = drainage + cond[layers - 1] * moisture[layers - 1]
        for k in range(layers):
            out_ref[k, rows, :] = moisture[k]
        runoff_ref[rows, :] = wet_ref[rows, :] * (SOIL_STEPS * surface_ref[rows, :] + drainage)
        return carry

    lax.fori_loop(0, groups, one_group, 0)


def soil_update(forcing, land_mask, conductance, soil_moisture):
    wetness = land_mask.astype(jnp.float32)
    source = wetness * (
        jax.nn.softplus(forcing[0]) * jax.nn.sigmoid(forcing[1])
        - 0.5 * jax.nn.sigmoid(forcing[2]) * jax.nn.softplus(forcing[3])
    )
    surface = wetness * jax.nn.softplus(forcing[0]) * (1.0 - jax.nn.sigmoid(forcing[1]))
    layers, cells = conductance.shape
    rows = cells // 128
    grid = 2
    block = rows // grid
    plane = pl.BlockSpec((block, 128), lambda i: (i, 0))
    stack = pl.BlockSpec((layers, block, 128), lambda i: (0, i, 0))
    moisture, runoff = pl.pallas_call(
        soil_kernel,
        grid=(grid,),
        in_specs=[plane, plane, plane, stack, stack],
        out_specs=[stack, plane],
        out_shape=[
            jax.ShapeDtypeStruct((layers, rows, 128), jnp.float32),
            jax.ShapeDtypeStruct((rows, 128), jnp.float32),
        ],
    )(
        source.reshape(rows, 128),
        surface.reshape(rows, 128),
        wetness.reshape(rows, 128),
        conductance.reshape(layers, rows, 128),
        soil_moisture.reshape(layers, rows, 128),
    )
    return (moisture.reshape(layers, cells), runoff.reshape(cells))


CAP_P = 4
CAP_R = 2


def route_partials(flat_terms, pair_land, tile_count, sub_count, tile_index, sub_index):
    pair_count, width = flat_terms.shape
    owner_device = pair_land // LB_DEV
    tile_step = (owner_device // sub_count - tile_index + 1 + tile_count) % tile_count
    sub_step = (owner_device % sub_count - sub_index + sub_count) % sub_count
    group_count = 3 * sub_count
    group_id = tile_step * sub_count + sub_step
    hits = (group_id[:, None] == jnp.arange(group_count, dtype=jnp.int32)[None, :]).astype(jnp.int32)
    ranks = jnp.sum((jnp.cumsum(hits, axis=0) - hits) * hits, axis=1)
    slot_id = group_id * CAP_P + ranks
    slot_count = group_count * CAP_P
    placing = slot_id[None, :] == jnp.arange(slot_count, dtype=jnp.int32)[:, None]
    source = jnp.sum(jnp.where(placing, jnp.arange(pair_count, dtype=jnp.int32)[None, :] + 1, 0), axis=1) - 1
    filled = source >= 0
    picked = jnp.maximum(source, 0)
    rows = jnp.where(filled[:, None], flat_terms[picked], 0.0)
    ids = jnp.where(filled, pair_land[picked] % LB_DEV, -1).astype(jnp.float32)
    ids = jnp.pad(ids.reshape(group_count, CAP_P), ((0, 0), (0, 128 - CAP_P)))
    messages = jnp.concatenate([rows.reshape(group_count, CAP_P * width), ids], axis=1)
    devices = tile_count * sub_count
    received = []
    for tile_offset in range(3):
        for sub_offset in range(sub_count):
            message = messages[tile_offset * sub_count + sub_offset]
            if tile_offset == 1 and sub_offset == 0:
                received.append(message)
                continue
            route = []
            for d in range(devices):
                t, s = divmod(d, sub_count)
                target = ((t + tile_offset - 1) % tile_count) * sub_count + (s + sub_offset) % sub_count
                route.append((d, target))
            received.append(lax.ppermute(message, ("tile", "sub"), route))
    got = jnp.stack(received)
    data = got[:, : CAP_P * width].reshape(slot_count, width)
    got_ids = got[:, CAP_P * width : CAP_P * width + CAP_P].reshape(slot_count)
    selector = (got_ids[None, :] == jnp.arange(LB_DEV, dtype=jnp.float32)[:, None]).astype(jnp.float32)
    return jnp.dot(selector, data, precision=lax.Precision.HIGHEST)


def on_device(
    atm_fields, pair_atm, pair_land, pair_weight, land_mask, conductance, soil_moisture, river_owner
):
    tile_count = lax.axis_size("tile")
    sub_count = lax.axis_size("sub")
    tile_index = lax.axis_index("tile")
    sub_index = lax.axis_index("sub")
    field_count, row_count, row_width = atm_fields.shape
    extended = padded(atm_fields, ((("tile", "sub"), 1),), 1)
    grad_x = x_gradient(atm_fields)
    grad_y = (extended[:, 2:, :] - extended[:, :-2, :]) * 0.5
    stacked = jnp.concatenate([atm_fields, grad_x, grad_y], axis=2).astype(jnp.bfloat16)
    pair_count = pair_atm.shape[0]
    picked = stacked[:, pair_atm, :]
    weights = pair_weight.reshape(pair_count, 3 * row_width, LBLK)
    partial_value = jnp.einsum("fpk,pkl->pfl", picked, weights, preferred_element_type=jnp.float32)
    flat_terms = partial_value.reshape(pair_count, field_count * LBLK)
    owned_sums = route_partials(flat_terms, pair_land, tile_count, sub_count, tile_index, sub_index)
    forcing = owned_sums.reshape(LB_DEV, field_count, LBLK).transpose(1, 0, 2).reshape(
        field_count, LB_DEV * LBLK
    )
    land_forcing = forcing.astype(jnp.bfloat16)
    moisture, runoff = soil_update(forcing, land_mask, conductance, soil_moisture)
    block_count = runoff.shape[0] // RBLK
    capacity = CAP_R
    runoff_blocks = runoff.reshape(block_count, RBLK)
    hits = (river_owner[:, None] == jnp.arange(tile_count, dtype=jnp.int32)[None, :]).astype(
        jnp.int32
    )
    ranks = jnp.sum((jnp.cumsum(hits, axis=0) - hits) * hits, axis=1)
    slot_id = river_owner * capacity + ranks
    placing = slot_id[None, :] == jnp.arange(tile_count * capacity, dtype=jnp.int32)[:, None]
    values = jnp.dot(placing.astype(jnp.float32), runoff_blocks, precision=lax.Precision.HIGHEST)
    values = values.reshape(tile_count, capacity * RBLK)
    block_ids = (tile_index * sub_count + sub_index) * block_count + jnp.arange(
        block_count, dtype=jnp.int32
    )
    numbers = jnp.sum(jnp.where(placing, block_ids[None, :] + 1, 0), axis=1) - 1
    numbers = numbers.astype(jnp.float32).reshape(tile_count, capacity)
    numbers = jnp.pad(numbers, ((0, 0), (0, RBLK - capacity)))
    packed = jnp.concatenate([values, numbers], axis=1)
    got = lax.all_to_all(packed, "tile", split_axis=0, concat_axis=0, tiled=True)
    river_runoff = got[:, : capacity * RBLK].reshape(tile_count, capacity, RBLK)[None, None]
    river_blocks = got[:, capacity * RBLK : capacity * RBLK + capacity].astype(jnp.int32)[None, None]
    return (land_forcing, moisture, river_runoff, river_blocks)


def solution(mesh):
    return jax.shard_map(
        on_device,
        mesh=mesh,
        in_specs=(
            P(None, ("tile", "sub"), None),
            P(("tile", "sub")),
            P(("tile", "sub")),
            P(("tile", "sub"), None, None, None),
            P(("tile", "sub")),
            P(None, ("tile", "sub")),
            P(None, ("tile", "sub")),
            P(("tile", "sub")),
        ),
        out_specs=(
            P(None, ("tile", "sub")),
            P(None, ("tile", "sub")),
            P("tile", "sub", None, None, None),
            P("tile", "sub", None, None),
        ),
        check_vma=False,
    )
```

```python
import jax
import jax.numpy as jnp
from jax import lax
from jax.sharding import PartitionSpec as P
from jax.experimental import pallas as pl
from jax.experimental.pallas import tpu as pltpu

SOIL_STEPS = 4
LBLK = 512
RBLK = 128
LB_DEV = 16


def passed_along(block, axis, distance):
    devices = range(lax.axis_size(axis))
    route = [((i - distance) % len(devices), i) for i in devices]
    return lax.ppermute(block, axis, route)


def padded(array, sides, width):
    for axis, dim in sides:
        devices, length = (lax.axis_size(axis), array.shape[dim])
        up = [(i, (i + 1) % devices) for i in range(devices)]
        down = [(j, i) for i, j in up]
        last = lax.slice_in_dim(array, length - width, length, axis=dim)
        initial = lax.slice_in_dim(array, 0, width, axis=dim)
        before = lax.ppermute(last, axis, up)
        after = lax.ppermute(initial, axis, down)
        array = jnp.concatenate([before, array, after], axis=dim)
    return array


def x_gradient(fields):
    inner = (fields[:, :, 2:] - fields[:, :, :-2]) * 0.5
    first = fields[:, :, 1:2] - fields[:, :, 0:1]
    last = fields[:, :, -1:] - fields[:, :, -2:-1]
    return jnp.concatenate([first, inner, last], axis=2)


def column_factors(conductance):
    layers = conductance.shape[0]
    inverse = []
    ratios = []
    for k in range(layers):
        diagonal = 1.0 + conductance[k]
        if k > 0:
            diagonal = (
                diagonal
                + conductance[k - 1]
                - conductance[k - 1] * conductance[k - 1] * inverse[k - 1]
            )
        pivot_inv = 1.0 / diagonal
        inverse.append(pivot_inv)
        ratios.append(-conductance[k] * pivot_inv)
    return (inverse, ratios)


def column_solve(moisture, source, conductance, inverse, ratios):
    layers = len(inverse)
    forward = []
    for k in range(layers):
        if k == 0:
            column_value = moisture[0] + source
        else:
            column_value = moisture[k] + conductance[k - 1] * forward[k - 1]
        forward.append(column_value * inverse[k])
    solved = [forward[layers - 1]]
    for k in range(layers - 2, -1, -1):
        solved.insert(0, forward[k] - ratios[k] * solved[0])
    return jnp.stack(solved)


def soil_kernel(source_ref, surface_ref, wet_ref, cond_ref, moist_ref, out_ref, runoff_ref):
    layers = cond_ref.shape[0]
    groups = cond_ref.shape[1] // 8

    def one_group(g, carry):
        rows = pl.ds(pl.multiple_of(g * 8, 8), 8)
        cond = [cond_ref[k, rows, :] for k in range(layers)]
        inverse = []
        ratios = []
        for k in range(layers):
            diagonal = 1.0 + cond[k]
            if k > 0:
                diagonal = diagonal + cond[k - 1] - cond[k - 1] * cond[k - 1] * inverse[k - 1]
            pivot_inv = 1.0 / diagonal
            inverse.append(pivot_inv)
            ratios.append(-cond[k] * pivot_inv)
        source = source_ref[rows, :]
        moisture = [moist_ref[k, rows, :] for k in range(layers)]
        drainage = jnp.zeros_like(source)
        for substep in range(SOIL_STEPS):
            forward = []
            for k in range(layers):
                if k == 0:
                    column_value = moisture[0] + source
                else:
                    column_value = moisture[k] + cond[k - 1] * forward[k - 1]
                forward.append(column_value * inverse[k])
            solved = [forward[layers - 1]]
            for k in range(layers - 2, -1, -1):
                solved.insert(0, forward[k] - ratios[k] * solved[0])
            moisture = solved
            drainage = drainage + cond[layers - 1] * moisture[layers - 1]
        for k in range(layers):
            out_ref[k, rows, :] = moisture[k]
        runoff_ref[rows, :] = wet_ref[rows, :] * (SOIL_STEPS * surface_ref[rows, :] + drainage)
        return carry

    lax.fori_loop(0, groups, one_group, 0)


def soil_update(forcing, land_mask, conductance, soil_moisture):
    wetness = land_mask.astype(jnp.float32)
    source = wetness * (
        jax.nn.softplus(forcing[0]) * jax.nn.sigmoid(forcing[1])
        - 0.5 * jax.nn.sigmoid(forcing[2]) * jax.nn.softplus(forcing[3])
    )
    surface = wetness * jax.nn.softplus(forcing[0]) * (1.0 - jax.nn.sigmoid(forcing[1]))
    layers, cells = conductance.shape
    rows = cells // 128
    grid = 2
    block = rows // grid
    plane = pl.BlockSpec((block, 128), lambda i: (i, 0))
    stack = pl.BlockSpec((layers, block, 128), lambda i: (0, i, 0))
    moisture, runoff = pl.pallas_call(
        soil_kernel,
        grid=(grid,),
        in_specs=[plane, plane, plane, stack, stack],
        out_specs=[stack, plane],
        out_shape=[
            jax.ShapeDtypeStruct((layers, rows, 128), jnp.float32),
            jax.ShapeDtypeStruct((rows, 128), jnp.float32),
        ],
    )(
        source.reshape(rows, 128),
        surface.reshape(rows, 128),
        wetness.reshape(rows, 128),
        conductance.reshape(layers, rows, 128),
        soil_moisture.reshape(layers, rows, 128),
    )
    return (moisture.reshape(layers, cells), runoff.reshape(cells))


CAP_P = 4
CAP_R = 2


def id_rows(ids, width):
    flat = ids.reshape(-1)
    return jnp.pad(flat, (0, 8 * width - flat.shape[0])).reshape(8, width)


def route_partials(partial_value, pair_land, tile_count, sub_count, tile_index):
    pair_count, field_count, width = partial_value.shape
    owner_device = pair_land // LB_DEV
    tile_step = (owner_device // sub_count - tile_index + 1 + tile_count) % tile_count
    dest_sub = owner_device % sub_count
    group_count = 3 * sub_count
    group_id = dest_sub * 3 + tile_step
    hits = (group_id[:, None] == jnp.arange(group_count, dtype=jnp.int32)[None, :]).astype(jnp.int32)
    ranks = jnp.sum((jnp.cumsum(hits, axis=0) - hits) * hits, axis=1)
    slot_id = group_id * CAP_P + ranks
    slot_count = group_count * CAP_P
    placing = slot_id[None, :] == jnp.arange(slot_count, dtype=jnp.int32)[:, None]
    source = jnp.sum(jnp.where(placing, jnp.arange(pair_count, dtype=jnp.int32)[None, :] + 1, 0), axis=1) - 1
    filled = source >= 0
    picked = jnp.maximum(source, 0)
    rows = jnp.where(filled[:, None, None], partial_value[picked], 0.0)
    ids = jnp.where(filled, pair_land[picked] % LB_DEV, -1).astype(jnp.float32)
    chunk_rows = 3 * CAP_P * field_count
    ids = ids.reshape(sub_count, 3 * CAP_P)
    chunks = jnp.concatenate(
        [
            rows.reshape(sub_count, chunk_rows, width),
            jnp.stack([id_rows(ids[j], width) for j in range(sub_count)]),
        ],
        axis=1,
    )
    by_sub = lax.all_to_all(chunks, "sub", split_axis=0, concat_axis=0, tiled=True)
    part_rows = CAP_P * field_count
    got_ids = by_sub[:, chunk_rows, : 3 * CAP_P]
    messages = []
    for tile_step in range(3):
        data = by_sub[:, tile_step * part_rows : (tile_step + 1) * part_rows, :]
        data = data.reshape(sub_count * part_rows, width)
        step_ids = got_ids[:, tile_step * CAP_P : (tile_step + 1) * CAP_P]
        messages.append(jnp.concatenate([data, id_rows(step_ids, width)], axis=0))
    devices = range(tile_count)
    received = [
        lax.ppermute(messages[0], "tile", [(i, (i - 1) % tile_count) for i in devices]),
        messages[1],
        lax.ppermute(messages[2], "tile", [(i, (i + 1) % tile_count) for i in devices]),
    ]
    message_rows = sub_count * part_rows
    data = jnp.concatenate([m[:message_rows] for m in received], axis=0)
    slot_ids = jnp.concatenate([m[message_rows, : sub_count * CAP_P] for m in received])
    selector = (slot_ids[None, :] == jnp.arange(LB_DEV, dtype=jnp.float32)[:, None]).astype(jnp.float32)
    data = data.reshape(slot_ids.shape[0], field_count, width)
    return jnp.einsum("bs,sfl->fbl", selector, data, precision=lax.Precision.HIGHEST)


def on_device(
    atm_fields, pair_atm, pair_land, pair_weight, land_mask, conductance, soil_moisture, river_owner
):
    tile_count = lax.axis_size("tile")
    sub_count = lax.axis_size("sub")
    tile_index = lax.axis_index("tile")
    sub_index = lax.axis_index("sub")
    field_count, row_count, row_width = atm_fields.shape
    extended = padded(atm_fields, ((("tile", "sub"), 1),), 1)
    grad_x = x_gradient(atm_fields)
    grad_y = (extended[:, 2:, :] - extended[:, :-2, :]) * 0.5
    stacked = jnp.concatenate([atm_fields, grad_x, grad_y], axis=2).astype(jnp.bfloat16)
    pair_count = pair_atm.shape[0]
    picked = stacked[:, pair_atm, :]
    weights = pair_weight.reshape(pair_count, 3 * row_width, LBLK)
    partial_value = jnp.einsum("fpk,pkl->pfl", picked, weights, preferred_element_type=jnp.float32)
    owned_sums = route_partials(partial_value, pair_land, tile_count, sub_count, tile_index)
    forcing = owned_sums.reshape(field_count, LB_DEV * LBLK)
    land_forcing = forcing.astype(jnp.bfloat16)
    moisture, runoff = soil_update(forcing, land_mask, conductance, soil_moisture)
    block_count = runoff.shape[0] // RBLK
    capacity = CAP_R
    runoff_blocks = runoff.reshape(block_count, RBLK)
    hits = (river_owner[:, None] == jnp.arange(tile_count, dtype=jnp.int32)[None, :]).astype(
        jnp.int32
    )
    ranks = jnp.sum((jnp.cumsum(hits, axis=0) - hits) * hits, axis=1)
    slot_id = river_owner * capacity + ranks
    placing = slot_id[None, :] == jnp.arange(tile_count * capacity, dtype=jnp.int32)[:, None]
    values = jnp.dot(placing.astype(jnp.float32), runoff_blocks, precision=lax.Precision.HIGHEST)
    values = values.reshape(tile_count, capacity * RBLK)
    block_ids = (tile_index * sub_count + sub_index) * block_count + jnp.arange(
        block_count, dtype=jnp.int32
    )
    numbers = jnp.sum(jnp.where(placing, block_ids[None, :] + 1, 0), axis=1) - 1
    numbers = numbers.astype(jnp.float32).reshape(tile_count, capacity)
    numbers = jnp.pad(numbers, ((0, 0), (0, RBLK - capacity)))
    packed = jnp.concatenate([values, numbers], axis=1)
    got = lax.all_to_all(packed, "tile", split_axis=0, concat_axis=0, tiled=True)
    river_runoff = got[:, : capacity * RBLK].reshape(tile_count, capacity, RBLK)[None, None]
    river_blocks = got[:, capacity * RBLK : capacity * RBLK + capacity].astype(jnp.int32)[None, None]
    return (land_forcing, moisture, river_runoff, river_blocks)


def solution(mesh):
    return jax.shard_map(
        on_device,
        mesh=mesh,
        in_specs=(
            P(None, ("tile", "sub"), None),
            P(("tile", "sub")),
            P(("tile", "sub")),
            P(("tile", "sub"), None, None, None),
            P(("tile", "sub")),
            P(None, ("tile", "sub")),
            P(None, ("tile", "sub")),
            P(("tile", "sub")),
        ),
        out_specs=(
            P(None, ("tile", "sub")),
            P(None, ("tile", "sub")),
            P("tile", "sub", None, None, None),
            P("tile", "sub", None, None),
        ),
        check_vma=False,
    )
```

```python
import jax
import jax.numpy as jnp
from jax import lax
from jax.sharding import PartitionSpec as P
from jax.experimental import pallas as pl
from jax.experimental.pallas import tpu as pltpu

SOIL_STEPS = 4
LBLK = 512
RBLK = 128
LB_DEV = 16


def passed_along(block, axis, distance):
    devices = range(lax.axis_size(axis))
    route = [((i - distance) % len(devices), i) for i in devices]
    return lax.ppermute(block, axis, route)


def padded(array, sides, width):
    for axis, dim in sides:
        devices, length = (lax.axis_size(axis), array.shape[dim])
        up = [(i, (i + 1) % devices) for i in range(devices)]
        down = [(j, i) for i, j in up]
        last = lax.slice_in_dim(array, length - width, length, axis=dim)
        initial = lax.slice_in_dim(array, 0, width, axis=dim)
        before = lax.ppermute(last, axis, up)
        after = lax.ppermute(initial, axis, down)
        array = jnp.concatenate([before, array, after], axis=dim)
    return array


def x_gradient(fields):
    inner = (fields[:, :, 2:] - fields[:, :, :-2]) * 0.5
    first = fields[:, :, 1:2] - fields[:, :, 0:1]
    last = fields[:, :, -1:] - fields[:, :, -2:-1]
    return jnp.concatenate([first, inner, last], axis=2)


def column_factors(conductance):
    layers = conductance.shape[0]
    inverse = []
    ratios = []
    for k in range(layers):
        diagonal = 1.0 + conductance[k]
        if k > 0:
            diagonal = (
                diagonal
                + conductance[k - 1]
                - conductance[k - 1] * conductance[k - 1] * inverse[k - 1]
            )
        pivot_inv = 1.0 / diagonal
        inverse.append(pivot_inv)
        ratios.append(-conductance[k] * pivot_inv)
    return (inverse, ratios)


def column_solve(moisture, source, conductance, inverse, ratios):
    layers = len(inverse)
    forward = []
    for k in range(layers):
        if k == 0:
            column_value = moisture[0] + source
        else:
            column_value = moisture[k] + conductance[k - 1] * forward[k - 1]
        forward.append(column_value * inverse[k])
    solved = [forward[layers - 1]]
    for k in range(layers - 2, -1, -1):
        solved.insert(0, forward[k] - ratios[k] * solved[0])
    return jnp.stack(solved)


def soil_kernel(source_ref, surface_ref, wet_ref, cond_ref, moist_ref, out_ref, runoff_ref):
    layers = cond_ref.shape[0]
    groups = cond_ref.shape[1] // 8

    def one_group(g, carry):
        rows = pl.ds(pl.multiple_of(g * 8, 8), 8)
        cond = [cond_ref[k, rows, :] for k in range(layers)]
        inverse = []
        ratios = []
        for k in range(layers):
            diagonal = 1.0 + cond[k]
            if k > 0:
                diagonal = diagonal + cond[k - 1] - cond[k - 1] * cond[k - 1] * inverse[k - 1]
            pivot_inv = 1.0 / diagonal
            inverse.append(pivot_inv)
            ratios.append(-cond[k] * pivot_inv)
        source = source_ref[rows, :]
        moisture = [moist_ref[k, rows, :] for k in range(layers)]
        drainage = jnp.zeros_like(source)
        for substep in range(SOIL_STEPS):
            forward = []
            for k in range(layers):
                if k == 0:
                    column_value = moisture[0] + source
                else:
                    column_value = moisture[k] + cond[k - 1] * forward[k - 1]
                forward.append(column_value * inverse[k])
            solved = [forward[layers - 1]]
            for k in range(layers - 2, -1, -1):
                solved.insert(0, forward[k] - ratios[k] * solved[0])
            moisture = solved
            drainage = drainage + cond[layers - 1] * moisture[layers - 1]
        for k in range(layers):
            out_ref[k, rows, :] = moisture[k]
        runoff_ref[rows, :] = wet_ref[rows, :] * (SOIL_STEPS * surface_ref[rows, :] + drainage)
        return carry

    lax.fori_loop(0, groups, one_group, 0)


def soil_inputs(forcing, wetness):
    source = wetness * (
        jax.nn.softplus(forcing[0]) * jax.nn.sigmoid(forcing[1])
        - 0.5 * jax.nn.sigmoid(forcing[2]) * jax.nn.softplus(forcing[3])
    )
    surface = wetness * jax.nn.softplus(forcing[0]) * (1.0 - jax.nn.sigmoid(forcing[1]))
    return (source, surface)


def soil_update(source, surface, wetness, conductance, soil_moisture):
    layers, rows, lanes = conductance.shape
    grid = 2
    block = rows // grid
    plane = pl.BlockSpec((block, lanes), lambda i: (i, 0))
    stack = pl.BlockSpec((layers, block, lanes), lambda i: (0, i, 0))
    moisture, runoff = pl.pallas_call(
        soil_kernel,
        grid=(grid,),
        in_specs=[plane, plane, plane, stack, stack],
        out_specs=[stack, plane],
        out_shape=[
            jax.ShapeDtypeStruct((layers, rows, lanes), jnp.float32),
            jax.ShapeDtypeStruct((rows, lanes), jnp.float32),
        ],
    )(
        source.reshape(rows, lanes),
        surface.reshape(rows, lanes),
        wetness,
        conductance,
        soil_moisture,
    )
    return (moisture.reshape(layers, rows * lanes), runoff.reshape(rows * lanes))


CAP_P = 4
CAP_R = 2


def id_rows(ids, width):
    flat = ids.reshape(-1)
    return jnp.pad(flat, (0, 8 * width - flat.shape[0])).reshape(8, width)


def slot_plan(pair_land, tile_count, sub_count, tile_index):
    pair_count = pair_land.shape[0]
    owner_device = pair_land // LB_DEV
    tile_step = (owner_device // sub_count - tile_index + 1 + tile_count) % tile_count
    dest_sub = owner_device % sub_count
    group_count = 3 * sub_count
    group_id = dest_sub * 3 + tile_step
    hits = (group_id[:, None] == jnp.arange(group_count, dtype=jnp.int32)[None, :]).astype(jnp.int32)
    ranks = jnp.sum((jnp.cumsum(hits, axis=0) - hits) * hits, axis=1)
    slot_id = group_id * CAP_P + ranks
    slot_count = group_count * CAP_P
    placing = slot_id[None, :] == jnp.arange(slot_count, dtype=jnp.int32)[:, None]
    source = jnp.sum(jnp.where(placing, jnp.arange(pair_count, dtype=jnp.int32)[None, :] + 1, 0), axis=1) - 1
    filled = source >= 0
    picked = jnp.maximum(source, 0)
    ids = jnp.where(filled, pair_land[picked] % LB_DEV, -1).astype(jnp.float32)
    return (filled, picked, ids)


def route_partials(partial_value, plan, sub_count, tile_count):
    filled, picked, ids = plan
    pair_count, field_count, width = partial_value.shape
    rows = jnp.where(filled[:, None, None], partial_value[picked], 0.0)
    chunk_rows = 3 * CAP_P * field_count
    ids = ids.reshape(sub_count, 3 * CAP_P)
    chunks = jnp.concatenate(
        [
            rows.reshape(sub_count, chunk_rows, width),
            jnp.stack([id_rows(ids[j], width) for j in range(sub_count)]),
        ],
        axis=1,
    )
    by_sub = lax.all_to_all(chunks, "sub", split_axis=0, concat_axis=0, tiled=True)
    part_rows = CAP_P * field_count
    got_ids = by_sub[:, chunk_rows, : 3 * CAP_P]
    messages = []
    for tile_step in range(3):
        data = by_sub[:, tile_step * part_rows : (tile_step + 1) * part_rows, :]
        data = data.reshape(sub_count * part_rows, width)
        step_ids = got_ids[:, tile_step * CAP_P : (tile_step + 1) * CAP_P]
        messages.append(jnp.concatenate([data, id_rows(step_ids, width)], axis=0))
    devices = range(tile_count)
    received = [
        lax.ppermute(messages[0], "tile", [(i, (i - 1) % tile_count) for i in devices]),
        messages[1],
        lax.ppermute(messages[2], "tile", [(i, (i + 1) % tile_count) for i in devices]),
    ]
    message_rows = sub_count * part_rows
    data = jnp.concatenate([m[:message_rows] for m in received], axis=0)
    slot_ids = jnp.concatenate([m[message_rows, : sub_count * CAP_P] for m in received])
    selector = (slot_ids[None, :] == jnp.arange(LB_DEV, dtype=jnp.float32)[:, None]).astype(jnp.float32)
    data = data.reshape(slot_ids.shape[0], field_count, width)
    return jnp.einsum("bs,sfl->fbl", selector, data, precision=lax.Precision.HIGHEST)


def on_device(
    atm_fields, pair_atm, pair_land, pair_weight, land_mask, conductance, soil_moisture, river_owner
):
    tile_count = lax.axis_size("tile")
    sub_count = lax.axis_size("sub")
    tile_index = lax.axis_index("tile")
    sub_index = lax.axis_index("sub")
    field_count, row_count, row_width = atm_fields.shape
    pair_count = pair_atm.shape[0]
    layers, cell_count = conductance.shape
    tiles = (cell_count // RBLK, RBLK)

    plain = jnp.concatenate([atm_fields, x_gradient(atm_fields)], axis=2).astype(jnp.bfloat16)
    weights = pair_weight.reshape(pair_count, 3 * row_width, LBLK)
    partial_plain = jnp.einsum(
        "fpk,pkl->pfl",
        plain[:, pair_atm, :],
        weights[:, : 2 * row_width, :],
        preferred_element_type=jnp.float32,
    )
    plan = slot_plan(pair_land, tile_count, sub_count, tile_index)
    wetness = land_mask.astype(jnp.float32).reshape(tiles)
    cond_tiles = conductance.reshape((layers,) + tiles)
    moist_tiles = soil_moisture.reshape((layers,) + tiles)

    block_count = cell_count // RBLK
    capacity = CAP_R
    hits = (river_owner[:, None] == jnp.arange(tile_count, dtype=jnp.int32)[None, :]).astype(
        jnp.int32
    )
    ranks = jnp.sum((jnp.cumsum(hits, axis=0) - hits) * hits, axis=1)
    slot_id = river_owner * capacity + ranks
    placing = slot_id[None, :] == jnp.arange(tile_count * capacity, dtype=jnp.int32)[:, None]
    placing_f = placing.astype(jnp.float32)
    block_ids = (tile_index * sub_count + sub_index) * block_count + jnp.arange(
        block_count, dtype=jnp.int32
    )
    numbers = jnp.sum(jnp.where(placing, block_ids[None, :] + 1, 0), axis=1) - 1
    numbers = numbers.astype(jnp.float32).reshape(tile_count, capacity)
    numbers = jnp.pad(numbers, ((0, 0), (0, RBLK - capacity)))

    (atm_fields, partial_plain, plan, wetness, cond_tiles, moist_tiles, placing_f, numbers) = (
        lax.optimization_barrier(
            (atm_fields, partial_plain, plan, wetness, cond_tiles, moist_tiles, placing_f, numbers)
        )
    )

    extended = padded(atm_fields, ((("tile", "sub"), 1),), 1)
    grad_y = ((extended[:, 2:, :] - extended[:, :-2, :]) * 0.5).astype(jnp.bfloat16)
    partial_value = partial_plain + jnp.einsum(
        "fpk,pkl->pfl",
        grad_y[:, pair_atm, :],
        weights[:, 2 * row_width :, :],
        preferred_element_type=jnp.float32,
    )
    owned_sums = route_partials(partial_value, plan, sub_count, tile_count)
    forcing = owned_sums.reshape(field_count, LB_DEV * LBLK)
    land_forcing = forcing.astype(jnp.bfloat16)
    source, surface = soil_inputs(forcing, wetness.reshape(cell_count))
    moisture, runoff = soil_update(source, surface, wetness, cond_tiles, moist_tiles)
    runoff_blocks = runoff.reshape(block_count, RBLK)
    values = jnp.dot(placing_f, runoff_blocks, precision=lax.Precision.HIGHEST)
    values = values.reshape(tile_count, capacity * RBLK)
    packed = jnp.concatenate([values, numbers], axis=1)
    got = lax.all_to_all(packed, "tile", split_axis=0, concat_axis=0, tiled=True)
    river_runoff = got[:, : capacity * RBLK].reshape(tile_count, capacity, RBLK)[None, None]
    river_blocks = got[:, capacity * RBLK : capacity * RBLK + capacity].astype(jnp.int32)[None, None]
    return (land_forcing, moisture, river_runoff, river_blocks)


def solution(mesh):
    return jax.shard_map(
        on_device,
        mesh=mesh,
        in_specs=(
            P(None, ("tile", "sub"), None),
            P(("tile", "sub")),
            P(("tile", "sub")),
            P(("tile", "sub"), None, None, None),
            P(("tile", "sub")),
            P(None, ("tile", "sub")),
            P(None, ("tile", "sub")),
            P(("tile", "sub")),
        ),
        out_specs=(
            P(None, ("tile", "sub")),
            P(None, ("tile", "sub")),
            P("tile", "sub", None, None, None),
            P("tile", "sub", None, None),
        ),
        check_vma=False,
    )
```

```python
import jax
import jax.numpy as jnp
from jax import lax
from jax.sharding import PartitionSpec as P
from jax.experimental import pallas as pl
from jax.experimental.pallas import tpu as pltpu

SOIL_STEPS = 4
LBLK = 512
RBLK = 128
LB_DEV = 16


def passed_along(block, axis, distance):
    devices = range(lax.axis_size(axis))
    route = [((i - distance) % len(devices), i) for i in devices]
    return lax.ppermute(block, axis, route)


def padded(array, sides, width):
    for axis, dim in sides:
        devices, length = (lax.axis_size(axis), array.shape[dim])
        up = [(i, (i + 1) % devices) for i in range(devices)]
        down = [(j, i) for i, j in up]
        last = lax.slice_in_dim(array, length - width, length, axis=dim)
        initial = lax.slice_in_dim(array, 0, width, axis=dim)
        before = lax.ppermute(last, axis, up)
        after = lax.ppermute(initial, axis, down)
        array = jnp.concatenate([before, array, after], axis=dim)
    return array


def x_gradient(fields):
    inner = (fields[:, :, 2:] - fields[:, :, :-2]) * 0.5
    first = fields[:, :, 1:2] - fields[:, :, 0:1]
    last = fields[:, :, -1:] - fields[:, :, -2:-1]
    return jnp.concatenate([first, inner, last], axis=2)


def column_factors(conductance):
    layers = conductance.shape[0]
    inverse = []
    ratios = []
    for k in range(layers):
        diagonal = 1.0 + conductance[k]
        if k > 0:
            diagonal = (
                diagonal
                + conductance[k - 1]
                - conductance[k - 1] * conductance[k - 1] * inverse[k - 1]
            )
        pivot_inv = 1.0 / diagonal
        inverse.append(pivot_inv)
        ratios.append(-conductance[k] * pivot_inv)
    return (inverse, ratios)


def column_solve(moisture, source, conductance, inverse, ratios):
    layers = len(inverse)
    forward = []
    for k in range(layers):
        if k == 0:
            column_value = moisture[0] + source
        else:
            column_value = moisture[k] + conductance[k - 1] * forward[k - 1]
        forward.append(column_value * inverse[k])
    solved = [forward[layers - 1]]
    for k in range(layers - 2, -1, -1):
        solved.insert(0, forward[k] - ratios[k] * solved[0])
    return jnp.stack(solved)


def soil_kernel(source_ref, surface_ref, wet_ref, cond_ref, moist_ref, out_ref, runoff_ref):
    layers = cond_ref.shape[0]
    groups = cond_ref.shape[1] // 8

    def one_group(g, carry):
        rows = pl.ds(pl.multiple_of(g * 8, 8), 8)
        cond = [cond_ref[k, rows, :] for k in range(layers)]
        inverse = []
        ratios = []
        for k in range(layers):
            diagonal = 1.0 + cond[k]
            if k > 0:
                diagonal = diagonal + cond[k - 1] - cond[k - 1] * cond[k - 1] * inverse[k - 1]
            pivot_inv = 1.0 / diagonal
            inverse.append(pivot_inv)
            ratios.append(-cond[k] * pivot_inv)
        source = source_ref[rows, :]
        moisture = [moist_ref[k, rows, :] for k in range(layers)]
        drainage = jnp.zeros_like(source)
        for substep in range(SOIL_STEPS):
            forward = []
            for k in range(layers):
                if k == 0:
                    column_value = moisture[0] + source
                else:
                    column_value = moisture[k] + cond[k - 1] * forward[k - 1]
                forward.append(column_value * inverse[k])
            solved = [forward[layers - 1]]
            for k in range(layers - 2, -1, -1):
                solved.insert(0, forward[k] - ratios[k] * solved[0])
            moisture = solved
            drainage = drainage + cond[layers - 1] * moisture[layers - 1]
        for k in range(layers):
            out_ref[k, rows, :] = moisture[k]
        runoff_ref[rows, :] = wet_ref[rows, :] * (SOIL_STEPS * surface_ref[rows, :] + drainage)
        return carry

    lax.fori_loop(0, groups, one_group, 0)


def soil_update(forcing, land_mask, conductance, soil_moisture):
    wetness = land_mask.astype(jnp.float32)
    source = wetness * (
        jax.nn.softplus(forcing[0]) * jax.nn.sigmoid(forcing[1])
        - 0.5 * jax.nn.sigmoid(forcing[2]) * jax.nn.softplus(forcing[3])
    )
    surface = wetness * jax.nn.softplus(forcing[0]) * (1.0 - jax.nn.sigmoid(forcing[1]))
    layers, cells = conductance.shape
    rows = cells // 128
    grid = 2
    block = rows // grid
    plane = pl.BlockSpec((block, 128), lambda i: (i, 0))
    stack = pl.BlockSpec((layers, block, 128), lambda i: (0, i, 0))
    moisture, runoff = pl.pallas_call(
        soil_kernel,
        grid=(grid,),
        in_specs=[plane, plane, plane, stack, stack],
        out_specs=[stack, plane],
        out_shape=[
            jax.ShapeDtypeStruct((layers, rows, 128), jnp.float32),
            jax.ShapeDtypeStruct((rows, 128), jnp.float32),
        ],
    )(
        source.reshape(rows, 128),
        surface.reshape(rows, 128),
        wetness.reshape(rows, 128),
        conductance.reshape(layers, rows, 128),
        soil_moisture.reshape(layers, rows, 128),
    )
    return (moisture.reshape(layers, cells), runoff.reshape(cells))


CAP_P = 4
CAP_R = 2


def id_rows(ids, width):
    flat = ids.reshape(-1)
    return jnp.pad(flat, (0, 8 * width - flat.shape[0])).reshape(8, width)


def route_partials(partial_value, pair_land, tile_count, sub_count, tile_index):
    pair_count, field_count, width = partial_value.shape
    owner_device = pair_land // LB_DEV
    tile_step = (owner_device // sub_count - tile_index + 1 + tile_count) % tile_count
    dest_sub = owner_device % sub_count
    group_count = 3 * sub_count
    group_id = dest_sub * 3 + tile_step
    hits = (group_id[:, None] == jnp.arange(group_count, dtype=jnp.int32)[None, :]).astype(jnp.int32)
    ranks = jnp.sum((jnp.cumsum(hits, axis=0) - hits) * hits, axis=1)
    slot_id = group_id * CAP_P + ranks
    slot_count = group_count * CAP_P
    placing = slot_id[None, :] == jnp.arange(slot_count, dtype=jnp.int32)[:, None]
    source = jnp.sum(jnp.where(placing, jnp.arange(pair_count, dtype=jnp.int32)[None, :] + 1, 0), axis=1) - 1
    filled = source >= 0
    picked = jnp.maximum(source, 0)
    rows = jnp.where(filled[:, None, None], partial_value[picked], 0.0)
    ids = jnp.where(filled, pair_land[picked] % LB_DEV, -1).astype(jnp.float32)
    chunk_rows = 3 * CAP_P * field_count
    ids = ids.reshape(sub_count, 3 * CAP_P)
    chunks = jnp.concatenate(
        [
            rows.reshape(sub_count, chunk_rows, width),
            jnp.stack([id_rows(ids[j], width) for j in range(sub_count)]),
        ],
        axis=1,
    )
    by_sub = lax.all_to_all(chunks, "sub", split_axis=0, concat_axis=0, tiled=True)
    part_rows = CAP_P * field_count
    got_ids = by_sub[:, chunk_rows, : 3 * CAP_P]
    messages = []
    for tile_step in range(3):
        data = by_sub[:, tile_step * part_rows : (tile_step + 1) * part_rows, :]
        data = data.reshape(sub_count * part_rows, width)
        step_ids = got_ids[:, tile_step * CAP_P : (tile_step + 1) * CAP_P]
        messages.append(jnp.concatenate([data, id_rows(step_ids, width)], axis=0))
    devices = range(tile_count)
    received = [
        lax.ppermute(messages[0], "tile", [(i, (i - 1) % tile_count) for i in devices]),
        messages[1],
        lax.ppermute(messages[2], "tile", [(i, (i + 1) % tile_count) for i in devices]),
    ]
    message_rows = sub_count * part_rows
    data = jnp.concatenate([m[:message_rows] for m in received], axis=0)
    slot_ids = jnp.concatenate([m[message_rows, : sub_count * CAP_P] for m in received])
    selector = (slot_ids[None, :] == jnp.arange(LB_DEV, dtype=jnp.float32)[:, None]).astype(jnp.float32)
    data = data.reshape(slot_ids.shape[0], field_count, width)
    return jnp.einsum("bs,sfl->fbl", selector, data, precision=lax.Precision.HIGHEST)


def on_device(
    atm_fields, pair_atm, pair_land, pair_weight, land_mask, conductance, soil_moisture, river_owner
):
    tile_count = lax.axis_size("tile")
    sub_count = lax.axis_size("sub")
    tile_index = lax.axis_index("tile")
    sub_index = lax.axis_index("sub")
    field_count, row_count, row_width = atm_fields.shape
    pair_count = pair_atm.shape[0]
    owners = river_owner.shape[0]
    small = lax.optimization_barrier(jnp.concatenate([pair_atm, pair_land, river_owner]))
    pair_atm = small[:pair_count]
    pair_land = small[pair_count : 2 * pair_count]
    river_owner = small[2 * pair_count : 2 * pair_count + owners]
    local_rows = lax.optimization_barrier(jnp.pad(atm_fields, ((0, 0), (0, 0), (0, row_width))))
    atm_fields = local_rows[:, :, :row_width]
    extended = padded(atm_fields, ((("tile", "sub"), 1),), 1)
    grad_x = x_gradient(atm_fields)
    grad_y = (extended[:, 2:, :] - extended[:, :-2, :]) * 0.5
    stacked = jnp.concatenate([atm_fields, grad_x, grad_y], axis=2).astype(jnp.bfloat16)
    picked = stacked[:, pair_atm, :]
    weights = pair_weight.reshape(pair_count, 3 * row_width, LBLK)
    partial_value = jnp.einsum("fpk,pkl->pfl", picked, weights, preferred_element_type=jnp.float32)
    owned_sums = route_partials(partial_value, pair_land, tile_count, sub_count, tile_index)
    forcing = owned_sums.reshape(field_count, LB_DEV * LBLK)
    land_forcing = forcing.astype(jnp.bfloat16)
    moisture, runoff = soil_update(forcing, land_mask, conductance, soil_moisture)
    block_count = runoff.shape[0] // RBLK
    capacity = CAP_R
    runoff_blocks = runoff.reshape(block_count, RBLK)
    hits = (river_owner[:, None] == jnp.arange(tile_count, dtype=jnp.int32)[None, :]).astype(
        jnp.int32
    )
    ranks = jnp.sum((jnp.cumsum(hits, axis=0) - hits) * hits, axis=1)
    slot_id = river_owner * capacity + ranks
    placing = slot_id[None, :] == jnp.arange(tile_count * capacity, dtype=jnp.int32)[:, None]
    values = jnp.dot(placing.astype(jnp.float32), runoff_blocks, precision=lax.Precision.HIGHEST)
    values = values.reshape(tile_count, capacity * RBLK)
    block_ids = (tile_index * sub_count + sub_index) * block_count + jnp.arange(
        block_count, dtype=jnp.int32
    )
    numbers = jnp.sum(jnp.where(placing, block_ids[None, :] + 1, 0), axis=1) - 1
    numbers = numbers.astype(jnp.float32).reshape(tile_count, capacity)
    numbers = jnp.pad(numbers, ((0, 0), (0, RBLK - capacity)))
    packed = jnp.concatenate([values, numbers], axis=1)
    got = lax.all_to_all(packed, "tile", split_axis=0, concat_axis=0, tiled=True)
    river_runoff = got[:, : capacity * RBLK].reshape(tile_count, capacity, RBLK)[None, None]
    river_blocks = got[:, capacity * RBLK : capacity * RBLK + capacity].astype(jnp.int32)[None, None]
    return (land_forcing, moisture, river_runoff, river_blocks)


def solution(mesh):
    return jax.shard_map(
        on_device,
        mesh=mesh,
        in_specs=(
            P(None, ("tile", "sub"), None),
            P(("tile", "sub")),
            P(("tile", "sub")),
            P(("tile", "sub"), None, None, None),
            P(("tile", "sub")),
            P(None, ("tile", "sub")),
            P(None, ("tile", "sub")),
            P(("tile", "sub")),
        ),
        out_specs=(
            P(None, ("tile", "sub")),
            P(None, ("tile", "sub")),
            P("tile", "sub", None, None, None),
            P("tile", "sub", None, None),
        ),
        check_vma=False,
    )
```

```python
import jax
import jax.numpy as jnp
from jax import lax
from jax.sharding import PartitionSpec as P
from jax.experimental import pallas as pl
from jax.experimental.pallas import tpu as pltpu

SOIL_STEPS = 4
LBLK = 512
RBLK = 128
LB_DEV = 16


def passed_along(block, axis, distance):
    devices = range(lax.axis_size(axis))
    route = [((i - distance) % len(devices), i) for i in devices]
    return lax.ppermute(block, axis, route)


def padded(array, sides, width):
    for axis, dim in sides:
        devices, length = (lax.axis_size(axis), array.shape[dim])
        up = [(i, (i + 1) % devices) for i in range(devices)]
        down = [(j, i) for i, j in up]
        last = lax.slice_in_dim(array, length - width, length, axis=dim)
        initial = lax.slice_in_dim(array, 0, width, axis=dim)
        before = lax.ppermute(last, axis, up)
        after = lax.ppermute(initial, axis, down)
        array = jnp.concatenate([before, array, after], axis=dim)
    return array


def x_gradient(fields):
    inner = (fields[:, :, 2:] - fields[:, :, :-2]) * 0.5
    first = fields[:, :, 1:2] - fields[:, :, 0:1]
    last = fields[:, :, -1:] - fields[:, :, -2:-1]
    return jnp.concatenate([first, inner, last], axis=2)


def column_factors(conductance):
    layers = conductance.shape[0]
    inverse = []
    ratios = []
    for k in range(layers):
        diagonal = 1.0 + conductance[k]
        if k > 0:
            diagonal = (
                diagonal
                + conductance[k - 1]
                - conductance[k - 1] * conductance[k - 1] * inverse[k - 1]
            )
        pivot_inv = 1.0 / diagonal
        inverse.append(pivot_inv)
        ratios.append(-conductance[k] * pivot_inv)
    return (inverse, ratios)


def column_solve(moisture, source, conductance, inverse, ratios):
    layers = len(inverse)
    forward = []
    for k in range(layers):
        if k == 0:
            column_value = moisture[0] + source
        else:
            column_value = moisture[k] + conductance[k - 1] * forward[k - 1]
        forward.append(column_value * inverse[k])
    solved = [forward[layers - 1]]
    for k in range(layers - 2, -1, -1):
        solved.insert(0, forward[k] - ratios[k] * solved[0])
    return jnp.stack(solved)


def factor_kernel(cond_ref, inverse_ref, ratio_ref):
    layers = cond_ref.shape[0]
    groups = cond_ref.shape[1] // 8

    def one_group(g, carry):
        rows = pl.ds(pl.multiple_of(g * 8, 8), 8)
        previous_cond = None
        previous_inv = None
        for k in range(layers):
            cond = cond_ref[k, rows, :]
            diagonal = 1.0 + cond
            if k > 0:
                diagonal = diagonal + previous_cond - previous_cond * previous_cond * previous_inv
            pivot_inv = 1.0 / diagonal
            inverse_ref[k, rows, :] = pivot_inv
            ratio_ref[k, rows, :] = -cond * pivot_inv
            previous_cond = cond
            previous_inv = pivot_inv
        return carry

    lax.fori_loop(0, groups, one_group, 0)


def soil_kernel(
    source_ref, surface_ref, wet_ref, cond_ref, inverse_ref, ratio_ref, moist_ref, out_ref, runoff_ref
):
    layers = cond_ref.shape[0]
    groups = cond_ref.shape[1] // 8

    def one_group(g, carry):
        rows = pl.ds(pl.multiple_of(g * 8, 8), 8)
        cond = [cond_ref[k, rows, :] for k in range(layers)]
        inverse = [inverse_ref[k, rows, :] for k in range(layers)]
        ratios = [ratio_ref[k, rows, :] for k in range(layers)]
        source = source_ref[rows, :]
        moisture = [moist_ref[k, rows, :] for k in range(layers)]
        drainage = jnp.zeros_like(source)
        for substep in range(SOIL_STEPS):
            forward = []
            for k in range(layers):
                if k == 0:
                    column_value = moisture[0] + source
                else:
                    column_value = moisture[k] + cond[k - 1] * forward[k - 1]
                forward.append(column_value * inverse[k])
            solved = [forward[layers - 1]]
            for k in range(layers - 2, -1, -1):
                solved.insert(0, forward[k] - ratios[k] * solved[0])
            moisture = solved
            drainage = drainage + cond[layers - 1] * moisture[layers - 1]
        for k in range(layers):
            out_ref[k, rows, :] = moisture[k]
        runoff_ref[rows, :] = wet_ref[rows, :] * (SOIL_STEPS * surface_ref[rows, :] + drainage)
        return carry

    lax.fori_loop(0, groups, one_group, 0)


def soil_update(forcing, land_mask, conductance, soil_moisture):
    wetness = land_mask.astype(jnp.float32)
    source = wetness * (
        jax.nn.softplus(forcing[0]) * jax.nn.sigmoid(forcing[1])
        - 0.5 * jax.nn.sigmoid(forcing[2]) * jax.nn.softplus(forcing[3])
    )
    surface = wetness * jax.nn.softplus(forcing[0]) * (1.0 - jax.nn.sigmoid(forcing[1]))
    layers, cells = conductance.shape
    rows = cells // 128
    grid = 2
    block = rows // grid
    plane = pl.BlockSpec((block, 128), lambda i: (i, 0))
    stack = pl.BlockSpec((layers, block, 128), lambda i: (0, i, 0))
    cond_tiles = conductance.reshape(layers, rows, 128)
    layer_shape = jax.ShapeDtypeStruct((layers, rows, 128), jnp.float32)
    inverse, ratios = pl.pallas_call(
        factor_kernel,
        grid=(grid,),
        in_specs=[stack],
        out_specs=[stack, stack],
        out_shape=[layer_shape, layer_shape],
    )(cond_tiles)
    moisture, runoff = pl.pallas_call(
        soil_kernel,
        grid=(grid,),
        in_specs=[plane, plane, plane, stack, stack, stack, stack],
        out_specs=[stack, plane],
        out_shape=[layer_shape, jax.ShapeDtypeStruct((rows, 128), jnp.float32)],
    )(
        source.reshape(rows, 128),
        surface.reshape(rows, 128),
        wetness.reshape(rows, 128),
        cond_tiles,
        inverse,
        ratios,
        soil_moisture.reshape(layers, rows, 128),
    )
    return (moisture.reshape(layers, cells), runoff.reshape(cells))


CAP_P = 4
CAP_R = 2


def id_rows(ids, width):
    flat = ids.reshape(-1)
    return jnp.pad(flat, (0, 8 * width - flat.shape[0])).reshape(8, width)


def route_partials(partial_value, pair_land, tile_count, sub_count, tile_index):
    pair_count, field_count, width = partial_value.shape
    owner_device = pair_land // LB_DEV
    tile_step = (owner_device // sub_count - tile_index + 1 + tile_count) % tile_count
    dest_sub = owner_device % sub_count
    group_count = 3 * sub_count
    group_id = dest_sub * 3 + tile_step
    hits = (group_id[:, None] == jnp.arange(group_count, dtype=jnp.int32)[None, :]).astype(jnp.int32)
    ranks = jnp.sum((jnp.cumsum(hits, axis=0) - hits) * hits, axis=1)
    slot_id = group_id * CAP_P + ranks
    slot_count = group_count * CAP_P
    placing = slot_id[None, :] == jnp.arange(slot_count, dtype=jnp.int32)[:, None]
    source = jnp.sum(jnp.where(placing, jnp.arange(pair_count, dtype=jnp.int32)[None, :] + 1, 0), axis=1) - 1
    filled = source >= 0
    picked = jnp.maximum(source, 0)
    rows = jnp.where(filled[:, None, None], partial_value[picked], 0.0)
    ids = jnp.where(filled, pair_land[picked] % LB_DEV, -1).astype(jnp.float32)
    chunk_rows = 3 * CAP_P * field_count
    ids = ids.reshape(sub_count, 3 * CAP_P)
    chunks = jnp.concatenate(
        [
            rows.reshape(sub_count, chunk_rows, width),
            jnp.stack([id_rows(ids[j], width) for j in range(sub_count)]),
        ],
        axis=1,
    )
    by_sub = lax.all_to_all(chunks, "sub", split_axis=0, concat_axis=0, tiled=True)
    part_rows = CAP_P * field_count
    got_ids = by_sub[:, chunk_rows, : 3 * CAP_P]
    messages = []
    for tile_step in range(3):
        data = by_sub[:, tile_step * part_rows : (tile_step + 1) * part_rows, :]
        data = data.reshape(sub_count * part_rows, width)
        step_ids = got_ids[:, tile_step * CAP_P : (tile_step + 1) * CAP_P]
        messages.append(jnp.concatenate([data, id_rows(step_ids, width)], axis=0))
    devices = range(tile_count)
    received = [
        lax.ppermute(messages[0], "tile", [(i, (i - 1) % tile_count) for i in devices]),
        messages[1],
        lax.ppermute(messages[2], "tile", [(i, (i + 1) % tile_count) for i in devices]),
    ]
    message_rows = sub_count * part_rows
    data = jnp.concatenate([m[:message_rows] for m in received], axis=0)
    slot_ids = jnp.concatenate([m[message_rows, : sub_count * CAP_P] for m in received])
    selector = (slot_ids[None, :] == jnp.arange(LB_DEV, dtype=jnp.float32)[:, None]).astype(jnp.float32)
    data = data.reshape(slot_ids.shape[0], field_count, width)
    return jnp.einsum("bs,sfl->fbl", selector, data, precision=lax.Precision.HIGHEST)


def on_device(
    atm_fields, pair_atm, pair_land, pair_weight, land_mask, conductance, soil_moisture, river_owner
):
    tile_count = lax.axis_size("tile")
    sub_count = lax.axis_size("sub")
    tile_index = lax.axis_index("tile")
    sub_index = lax.axis_index("sub")
    field_count, row_count, row_width = atm_fields.shape
    pair_count = pair_atm.shape[0]
    owners = river_owner.shape[0]
    small = lax.optimization_barrier(jnp.concatenate([pair_atm, pair_land, river_owner]))
    pair_atm = small[:pair_count]
    pair_land = small[pair_count : 2 * pair_count]
    river_owner = small[2 * pair_count : 2 * pair_count + owners]
    local_rows = lax.optimization_barrier(jnp.pad(atm_fields, ((0, 0), (0, 0), (0, row_width))))
    atm_fields = local_rows[:, :, :row_width]
    extended = padded(atm_fields, ((("tile", "sub"), 1),), 1)
    grad_x = x_gradient(atm_fields)
    grad_y = (extended[:, 2:, :] - extended[:, :-2, :]) * 0.5
    stacked = jnp.concatenate([atm_fields, grad_x, grad_y], axis=2).astype(jnp.bfloat16)
    picked = stacked[:, pair_atm, :]
    weights = pair_weight.reshape(pair_count, 3 * row_width, LBLK)
    partial_value = jnp.einsum("fpk,pkl->pfl", picked, weights, preferred_element_type=jnp.float32)
    owned_sums = route_partials(partial_value, pair_land, tile_count, sub_count, tile_index)
    forcing = owned_sums.reshape(field_count, LB_DEV * LBLK)
    land_forcing = forcing.astype(jnp.bfloat16)
    moisture, runoff = soil_update(forcing, land_mask, conductance, soil_moisture)
    block_count = runoff.shape[0] // RBLK
    capacity = CAP_R
    runoff_blocks = runoff.reshape(block_count, RBLK)
    hits = (river_owner[:, None] == jnp.arange(tile_count, dtype=jnp.int32)[None, :]).astype(
        jnp.int32
    )
    ranks = jnp.sum((jnp.cumsum(hits, axis=0) - hits) * hits, axis=1)
    slot_id = river_owner * capacity + ranks
    placing = slot_id[None, :] == jnp.arange(tile_count * capacity, dtype=jnp.int32)[:, None]
    values = jnp.dot(placing.astype(jnp.float32), runoff_blocks, precision=lax.Precision.HIGHEST)
    values = values.reshape(tile_count, capacity * RBLK)
    block_ids = (tile_index * sub_count + sub_index) * block_count + jnp.arange(
        block_count, dtype=jnp.int32
    )
    numbers = jnp.sum(jnp.where(placing, block_ids[None, :] + 1, 0), axis=1) - 1
    numbers = numbers.astype(jnp.float32).reshape(tile_count, capacity)
    numbers = jnp.pad(numbers, ((0, 0), (0, RBLK - capacity)))
    packed = jnp.concatenate([values, numbers], axis=1)
    got = lax.all_to_all(packed, "tile", split_axis=0, concat_axis=0, tiled=True)
    river_runoff = got[:, : capacity * RBLK].reshape(tile_count, capacity, RBLK)[None, None]
    river_blocks = got[:, capacity * RBLK : capacity * RBLK + capacity].astype(jnp.int32)[None, None]
    return (land_forcing, moisture, river_runoff, river_blocks)


def solution(mesh):
    return jax.shard_map(
        on_device,
        mesh=mesh,
        in_specs=(
            P(None, ("tile", "sub"), None),
            P(("tile", "sub")),
            P(("tile", "sub")),
            P(("tile", "sub"), None, None, None),
            P(("tile", "sub")),
            P(None, ("tile", "sub")),
            P(None, ("tile", "sub")),
            P(("tile", "sub")),
        ),
        out_specs=(
            P(None, ("tile", "sub")),
            P(None, ("tile", "sub")),
            P("tile", "sub", None, None, None),
            P("tile", "sub", None, None),
        ),
        check_vma=False,
    )
```

```python
import jax
import jax.numpy as jnp
from jax import lax
from jax.sharding import PartitionSpec as P
from jax.experimental import pallas as pl
from jax.experimental.pallas import tpu as pltpu

SOIL_STEPS = 4
LBLK = 512
RBLK = 128
LB_DEV = 16


def passed_along(block, axis, distance):
    devices = range(lax.axis_size(axis))
    route = [((i - distance) % len(devices), i) for i in devices]
    return lax.ppermute(block, axis, route)


def padded(array, sides, width):
    for axis, dim in sides:
        devices, length = (lax.axis_size(axis), array.shape[dim])
        up = [(i, (i + 1) % devices) for i in range(devices)]
        down = [(j, i) for i, j in up]
        last = lax.slice_in_dim(array, length - width, length, axis=dim)
        initial = lax.slice_in_dim(array, 0, width, axis=dim)
        before = lax.ppermute(last, axis, up)
        after = lax.ppermute(initial, axis, down)
        array = jnp.concatenate([before, array, after], axis=dim)
    return array


def x_gradient(fields):
    inner = (fields[:, :, 2:] - fields[:, :, :-2]) * 0.5
    first = fields[:, :, 1:2] - fields[:, :, 0:1]
    last = fields[:, :, -1:] - fields[:, :, -2:-1]
    return jnp.concatenate([first, inner, last], axis=2)


def column_factors(conductance):
    layers = conductance.shape[0]
    inverse = []
    ratios = []
    for k in range(layers):
        diagonal = 1.0 + conductance[k]
        if k > 0:
            diagonal = (
                diagonal
                + conductance[k - 1]
                - conductance[k - 1] * conductance[k - 1] * inverse[k - 1]
            )
        pivot_inv = 1.0 / diagonal
        inverse.append(pivot_inv)
        ratios.append(-conductance[k] * pivot_inv)
    return (inverse, ratios)


def column_solve(moisture, source, conductance, inverse, ratios):
    layers = len(inverse)
    forward = []
    for k in range(layers):
        if k == 0:
            column_value = moisture[0] + source
        else:
            column_value = moisture[k] + conductance[k - 1] * forward[k - 1]
        forward.append(column_value * inverse[k])
    solved = [forward[layers - 1]]
    for k in range(layers - 2, -1, -1):
        solved.insert(0, forward[k] - ratios[k] * solved[0])
    return jnp.stack(solved)


def soil_kernel(source_ref, surface_ref, wet_ref, cond_ref, moist_ref, out_ref, runoff_ref):
    layers = cond_ref.shape[0]
    groups = cond_ref.shape[1] // 8

    def one_group(g, carry):
        rows = pl.ds(pl.multiple_of(g * 8, 8), 8)
        cond = [cond_ref[k, rows, :] for k in range(layers)]
        inverse = []
        ratios = []
        for k in range(layers):
            diagonal = 1.0 + cond[k]
            if k > 0:
                diagonal = diagonal + cond[k - 1] - cond[k - 1] * cond[k - 1] * inverse[k - 1]
            pivot_inv = 1.0 / diagonal
            inverse.append(pivot_inv)
            ratios.append(-cond[k] * pivot_inv)
        source = source_ref[rows, :]
        moisture = [moist_ref[k, rows, :] for k in range(layers)]
        drainage = jnp.zeros_like(source)
        for substep in range(SOIL_STEPS):
            forward = []
            for k in range(layers):
                if k == 0:
                    column_value = moisture[0] + source
                else:
                    column_value = moisture[k] + cond[k - 1] * forward[k - 1]
                forward.append(column_value * inverse[k])
            solved = [forward[layers - 1]]
            for k in range(layers - 2, -1, -1):
                solved.insert(0, forward[k] - ratios[k] * solved[0])
            moisture = solved
            drainage = drainage + cond[layers - 1] * moisture[layers - 1]
        for k in range(layers):
            out_ref[k, rows, :] = moisture[k]
        runoff_ref[rows, :] = wet_ref[rows, :] * (SOIL_STEPS * surface_ref[rows, :] + drainage)
        return carry

    lax.fori_loop(0, groups, one_group, 0)


def soil_update(forcing, land_mask, conductance, soil_moisture):
    wetness = land_mask.astype(jnp.float32)
    source = wetness * (
        jax.nn.softplus(forcing[0]) * jax.nn.sigmoid(forcing[1])
        - 0.5 * jax.nn.sigmoid(forcing[2]) * jax.nn.softplus(forcing[3])
    )
    surface = wetness * jax.nn.softplus(forcing[0]) * (1.0 - jax.nn.sigmoid(forcing[1]))
    layers, cells = conductance.shape
    rows = cells // 128
    grid = 2
    block = rows // grid
    plane = pl.BlockSpec((block, 128), lambda i: (i, 0))
    stack = pl.BlockSpec((layers, block, 128), lambda i: (0, i, 0))
    moisture, runoff = pl.pallas_call(
        soil_kernel,
        grid=(grid,),
        in_specs=[plane, plane, plane, stack, stack],
        out_specs=[stack, plane],
        out_shape=[
            jax.ShapeDtypeStruct((layers, rows, 128), jnp.float32),
            jax.ShapeDtypeStruct((rows, 128), jnp.float32),
        ],
    )(
        source.reshape(rows, 128),
        surface.reshape(rows, 128),
        wetness.reshape(rows, 128),
        conductance.reshape(layers, rows, 128),
        soil_moisture.reshape(layers, rows, 128),
    )
    return (moisture.reshape(layers, cells), runoff.reshape(cells))


CAP_P = 4
CAP_R = 2


def id_rows(ids, width):
    flat = ids.reshape(-1)
    return jnp.pad(flat, (0, 8 * width - flat.shape[0])).reshape(8, width)


def route_partials(partial_value, pair_land, tile_count, sub_count, tile_index):
    pair_count, field_count, width = partial_value.shape
    owner_device = pair_land // LB_DEV
    tile_step = (owner_device // sub_count - tile_index + 1 + tile_count) % tile_count
    dest_sub = owner_device % sub_count
    group_count = 3 * sub_count
    group_id = dest_sub * 3 + tile_step
    hits = (group_id[:, None] == jnp.arange(group_count, dtype=jnp.int32)[None, :]).astype(jnp.int32)
    ranks = jnp.sum((jnp.cumsum(hits, axis=0) - hits) * hits, axis=1)
    slot_id = group_id * CAP_P + ranks
    slot_count = group_count * CAP_P
    placing = slot_id[None, :] == jnp.arange(slot_count, dtype=jnp.int32)[:, None]
    source = jnp.sum(jnp.where(placing, jnp.arange(pair_count, dtype=jnp.int32)[None, :] + 1, 0), axis=1) - 1
    filled = source >= 0
    picked = jnp.maximum(source, 0)
    rows = jnp.where(filled[:, None, None], partial_value[picked], 0.0)
    ids = jnp.where(filled, pair_land[picked] % LB_DEV, -1).astype(jnp.float32)
    chunk_rows = 3 * CAP_P * field_count
    ids = ids.reshape(sub_count, 3 * CAP_P)
    chunks = jnp.concatenate(
        [
            rows.reshape(sub_count, chunk_rows, width),
            jnp.stack([id_rows(ids[j], width) for j in range(sub_count)]),
        ],
        axis=1,
    )
    by_sub = lax.all_to_all(chunks, "sub", split_axis=0, concat_axis=0, tiled=True)
    part_rows = CAP_P * field_count
    got_ids = by_sub[:, chunk_rows, : 3 * CAP_P]
    messages = []
    for tile_step in range(3):
        data = by_sub[:, tile_step * part_rows : (tile_step + 1) * part_rows, :]
        data = data.reshape(sub_count * part_rows, width)
        step_ids = got_ids[:, tile_step * CAP_P : (tile_step + 1) * CAP_P]
        messages.append(jnp.concatenate([data, id_rows(step_ids, width)], axis=0))
    devices = range(tile_count)
    received = [
        lax.ppermute(messages[0], TILE, [(i, (i - 1) % tile_count) for i in devices]),
        messages[1],
        lax.ppermute(messages[2], TILE, [(i, (i + 1) % tile_count) for i in devices]),
    ]
    message_rows = sub_count * part_rows
    data = jnp.concatenate([m[:message_rows] for m in received], axis=0)
    slot_ids = jnp.concatenate([m[message_rows, : sub_count * CAP_P] for m in received])
    selector = (slot_ids[None, :] == jnp.arange(LB_DEV, dtype=jnp.float32)[:, None]).astype(jnp.float32)
    data = data.reshape(slot_ids.shape[0], field_count, width)
    return jnp.einsum("bs,sfl->fbl", selector, data, precision=lax.Precision.HIGHEST)


def on_device(
    atm_fields, pair_atm, pair_land, pair_weight, land_mask, conductance, soil_moisture, river_owner
):
    tile_count = lax.axis_size(TILE)
    sub_count = lax.axis_size("sub")
    tile_index = lax.axis_index(TILE)
    sub_index = lax.axis_index("sub")
    field_count, row_count, row_width = atm_fields.shape
    pair_count = pair_atm.shape[0]
    owners = river_owner.shape[0]
    small = lax.optimization_barrier(jnp.concatenate([pair_atm, pair_land, river_owner]))
    pair_atm = small[:pair_count]
    pair_land = small[pair_count : 2 * pair_count]
    river_owner = small[2 * pair_count : 2 * pair_count + owners]
    local_rows = lax.optimization_barrier(jnp.pad(atm_fields, ((0, 0), (0, 0), (0, row_width))))
    atm_fields = local_rows[:, :, :row_width]
    extended = padded(atm_fields, (((*TILE, "sub"), 1),), 1)
    grad_x = x_gradient(atm_fields)
    grad_y = (extended[:, 2:, :] - extended[:, :-2, :]) * 0.5
    stacked = jnp.concatenate([atm_fields, grad_x, grad_y], axis=2).astype(jnp.bfloat16)
    picked = stacked[:, pair_atm, :]
    weights = pair_weight.reshape(pair_count, 3 * row_width, LBLK)
    partial_value = jnp.einsum("fpk,pkl->pfl", picked, weights, preferred_element_type=jnp.float32)
    owned_sums = route_partials(partial_value, pair_land, tile_count, sub_count, tile_index)
    forcing = owned_sums.reshape(field_count, LB_DEV * LBLK)
    land_forcing = forcing.astype(jnp.bfloat16)
    moisture, runoff = soil_update(forcing, land_mask, conductance, soil_moisture)
    block_count = runoff.shape[0] // RBLK
    capacity = CAP_R
    runoff_blocks = runoff.reshape(block_count, RBLK)
    hits = (river_owner[:, None] == jnp.arange(tile_count, dtype=jnp.int32)[None, :]).astype(
        jnp.int32
    )
    ranks = jnp.sum((jnp.cumsum(hits, axis=0) - hits) * hits, axis=1)
    slot_id = river_owner * capacity + ranks
    placing = slot_id[None, :] == jnp.arange(tile_count * capacity, dtype=jnp.int32)[:, None]
    values = jnp.dot(placing.astype(jnp.float32), runoff_blocks, precision=lax.Precision.HIGHEST)
    values = values.reshape(tile_count, capacity * RBLK)
    block_ids = (tile_index * sub_count + sub_index) * block_count + jnp.arange(
        block_count, dtype=jnp.int32
    )
    numbers = jnp.sum(jnp.where(placing, block_ids[None, :] + 1, 0), axis=1) - 1
    numbers = numbers.astype(jnp.float32).reshape(tile_count, capacity)
    numbers = jnp.pad(numbers, ((0, 0), (0, RBLK - capacity)))
    packed = jnp.concatenate([values, numbers], axis=1)
    high = lax.axis_size("tile_hi")
    low = lax.axis_size("tile_lo")
    packed = packed.reshape(high, low, packed.shape[1]).transpose(1, 0, 2)
    packed = lax.all_to_all(packed, "tile_lo", split_axis=0, concat_axis=0, tiled=True)
    packed = packed.transpose(1, 0, 2)
    got = lax.all_to_all(packed, "tile_hi", split_axis=0, concat_axis=0, tiled=True)
    got = got.reshape(tile_count, got.shape[2])
    river_runoff = got[:, : capacity * RBLK].reshape(tile_count, capacity, RBLK)[None, None]
    river_blocks = got[:, capacity * RBLK : capacity * RBLK + capacity].astype(jnp.int32)[None, None]
    return (land_forcing, moisture, river_runoff, river_blocks)


TILE = ("tile_hi", "tile_lo")


def solution(mesh):
    tiles, subs = mesh.devices.shape
    low = 8 if tiles % 8 == 0 else tiles
    split_mesh = jax.sharding.Mesh(mesh.devices.reshape(tiles // low, low, subs), (*TILE, "sub"))
    lined = (*TILE, "sub")
    return jax.shard_map(
        on_device,
        mesh=split_mesh,
        in_specs=(
            P(None, lined, None),
            P(lined),
            P(lined),
            P(lined, None, None, None),
            P(lined),
            P(None, lined),
            P(None, lined),
            P(lined),
        ),
        out_specs=(
            P(None, lined),
            P(None, lined),
            P(TILE, "sub", None, None, None),
            P(TILE, "sub", None, None),
        ),
        check_vma=False,
    )
```

```python
import jax
import jax.numpy as jnp
from jax import lax
from jax.sharding import PartitionSpec as P
from jax.experimental import pallas as pl
from jax.experimental.pallas import tpu as pltpu

SOIL_STEPS = 4
LBLK = 512
RBLK = 128
LB_DEV = 16


def passed_along(block, axis, distance):
    devices = range(lax.axis_size(axis))
    route = [((i - distance) % len(devices), i) for i in devices]
    return lax.ppermute(block, axis, route)


def padded(array, sides, width):
    for axis, dim in sides:
        devices, length = (lax.axis_size(axis), array.shape[dim])
        up = [(i, (i + 1) % devices) for i in range(devices)]
        down = [(j, i) for i, j in up]
        last = lax.slice_in_dim(array, length - width, length, axis=dim)
        initial = lax.slice_in_dim(array, 0, width, axis=dim)
        before = lax.ppermute(last, axis, up)
        after = lax.ppermute(initial, axis, down)
        array = jnp.concatenate([before, array, after], axis=dim)
    return array


def x_gradient(fields):
    inner = (fields[:, :, 2:] - fields[:, :, :-2]) * 0.5
    first = fields[:, :, 1:2] - fields[:, :, 0:1]
    last = fields[:, :, -1:] - fields[:, :, -2:-1]
    return jnp.concatenate([first, inner, last], axis=2)


def column_factors(conductance):
    layers = conductance.shape[0]
    inverse = []
    ratios = []
    for k in range(layers):
        diagonal = 1.0 + conductance[k]
        if k > 0:
            diagonal = (
                diagonal
                + conductance[k - 1]
                - conductance[k - 1] * conductance[k - 1] * inverse[k - 1]
            )
        pivot_inv = 1.0 / diagonal
        inverse.append(pivot_inv)
        ratios.append(-conductance[k] * pivot_inv)
    return (inverse, ratios)


def column_solve(moisture, source, conductance, inverse, ratios):
    layers = len(inverse)
    forward = []
    for k in range(layers):
        if k == 0:
            column_value = moisture[0] + source
        else:
            column_value = moisture[k] + conductance[k - 1] * forward[k - 1]
        forward.append(column_value * inverse[k])
    solved = [forward[layers - 1]]
    for k in range(layers - 2, -1, -1):
        solved.insert(0, forward[k] - ratios[k] * solved[0])
    return jnp.stack(solved)


def soil_kernel(
    source_ref, surface_ref, wet_ref, cond_ref, moist_ref, out_ref, runoff_ref, inv_ref, ratio_ref
):
    layers = cond_ref.shape[0]
    groups = cond_ref.shape[1] // 32

    def one_group(g, carry):
        rows = pl.ds(pl.multiple_of(g * 32, 32), 32)
        previous_cond = None
        previous_inv = None
        for k in range(layers):
            cond = cond_ref[k, rows, :]
            diagonal = 1.0 + cond
            if k > 0:
                diagonal = diagonal + previous_cond - previous_cond * previous_cond * previous_inv
            pivot_inv = 1.0 / diagonal
            inv_ref[k] = pivot_inv
            ratio_ref[k] = -cond * pivot_inv
            previous_cond = cond
            previous_inv = pivot_inv
        source = source_ref[rows, :]
        moisture = [moist_ref[k, rows, :] for k in range(layers)]
        drainage = jnp.zeros_like(source)
        for substep in range(SOIL_STEPS):
            forward = []
            for k in range(layers):
                if k == 0:
                    column_value = moisture[0] + source
                else:
                    column_value = moisture[k] + cond_ref[k - 1, rows, :] * forward[k - 1]
                forward.append(column_value * inv_ref[k])
            solved = [forward[layers - 1]]
            for k in range(layers - 2, -1, -1):
                solved.insert(0, forward[k] - ratio_ref[k] * solved[0])
            moisture = solved
            drainage = drainage + cond_ref[layers - 1, rows, :] * moisture[layers - 1]
        for k in range(layers):
            out_ref[k, rows, :] = moisture[k]
        runoff_ref[rows, :] = wet_ref[rows, :] * (SOIL_STEPS * surface_ref[rows, :] + drainage)
        return carry

    lax.fori_loop(0, groups, one_group, 0)


def soil_update(forcing, land_mask, conductance, soil_moisture):
    wetness = land_mask.astype(jnp.float32)
    source = wetness * (
        jax.nn.softplus(forcing[0]) * jax.nn.sigmoid(forcing[1])
        - 0.5 * jax.nn.sigmoid(forcing[2]) * jax.nn.softplus(forcing[3])
    )
    surface = wetness * jax.nn.softplus(forcing[0]) * (1.0 - jax.nn.sigmoid(forcing[1]))
    layers, cells = conductance.shape
    rows = cells // 128
    grid = 2
    block = rows // grid
    plane = pl.BlockSpec((block, 128), lambda i: (i, 0))
    stack = pl.BlockSpec((layers, block, 128), lambda i: (0, i, 0))
    moisture, runoff = pl.pallas_call(
        soil_kernel,
        grid=(grid,),
        in_specs=[plane, plane, plane, stack, stack],
        out_specs=[stack, plane],
        scratch_shapes=[pltpu.VMEM((layers, 32, 128), jnp.float32)] * 2,
        out_shape=[
            jax.ShapeDtypeStruct((layers, rows, 128), jnp.float32),
            jax.ShapeDtypeStruct((rows, 128), jnp.float32),
        ],
    )(
        source.reshape(rows, 128),
        surface.reshape(rows, 128),
        wetness.reshape(rows, 128),
        conductance.reshape(layers, rows, 128),
        soil_moisture.reshape(layers, rows, 128),
    )
    return (moisture.reshape(layers, cells), runoff.reshape(cells))


CAP_P = 4
CAP_R = 2


def id_rows(ids, width):
    flat = ids.reshape(-1)
    return jnp.pad(flat, (0, 8 * width - flat.shape[0])).reshape(8, width)


def route_partials(partial_value, pair_land, tile_count, sub_count, tile_index):
    pair_count, field_count, width = partial_value.shape
    owner_device = pair_land // LB_DEV
    tile_step = (owner_device // sub_count - tile_index + 1 + tile_count) % tile_count
    dest_sub = owner_device % sub_count
    group_count = 3 * sub_count
    group_id = dest_sub * 3 + tile_step
    hits = (group_id[:, None] == jnp.arange(group_count, dtype=jnp.int32)[None, :]).astype(jnp.int32)
    ranks = jnp.sum((jnp.cumsum(hits, axis=0) - hits) * hits, axis=1)
    slot_id = group_id * CAP_P + ranks
    slot_count = group_count * CAP_P
    placing = slot_id[None, :] == jnp.arange(slot_count, dtype=jnp.int32)[:, None]
    source = jnp.sum(jnp.where(placing, jnp.arange(pair_count, dtype=jnp.int32)[None, :] + 1, 0), axis=1) - 1
    filled = source >= 0
    picked = jnp.maximum(source, 0)
    rows = jnp.where(filled[:, None, None], partial_value[picked], 0.0)
    ids = jnp.where(filled, pair_land[picked] % LB_DEV, -1).astype(jnp.float32)
    chunk_rows = 3 * CAP_P * field_count
    ids = ids.reshape(sub_count, 3 * CAP_P)
    chunks = jnp.concatenate(
        [
            rows.reshape(sub_count, chunk_rows, width),
            jnp.stack([id_rows(ids[j], width) for j in range(sub_count)]),
        ],
        axis=1,
    )
    by_sub = lax.all_to_all(chunks, "sub", split_axis=0, concat_axis=0, tiled=True)
    part_rows = CAP_P * field_count
    got_ids = by_sub[:, chunk_rows, : 3 * CAP_P]
    messages = []
    for tile_step in range(3):
        data = by_sub[:, tile_step * part_rows : (tile_step + 1) * part_rows, :]
        data = data.reshape(sub_count * part_rows, width)
        step_ids = got_ids[:, tile_step * CAP_P : (tile_step + 1) * CAP_P]
        messages.append(jnp.concatenate([data, id_rows(step_ids, width)], axis=0))
    devices = range(tile_count)
    received = [
        lax.ppermute(messages[0], "tile", [(i, (i - 1) % tile_count) for i in devices]),
        messages[1],
        lax.ppermute(messages[2], "tile", [(i, (i + 1) % tile_count) for i in devices]),
    ]
    message_rows = sub_count * part_rows
    data = jnp.concatenate([m[:message_rows] for m in received], axis=0)
    slot_ids = jnp.concatenate([m[message_rows, : sub_count * CAP_P] for m in received])
    selector = (slot_ids[None, :] == jnp.arange(LB_DEV, dtype=jnp.float32)[:, None]).astype(jnp.float32)
    data = data.reshape(slot_ids.shape[0], field_count, width)
    return jnp.einsum("bs,sfl->fbl", selector, data, precision=lax.Precision.HIGHEST)


def on_device(
    atm_fields, pair_atm, pair_land, pair_weight, land_mask, conductance, soil_moisture, river_owner
):
    tile_count = lax.axis_size("tile")
    sub_count = lax.axis_size("sub")
    tile_index = lax.axis_index("tile")
    sub_index = lax.axis_index("sub")
    field_count, row_count, row_width = atm_fields.shape
    pair_count = pair_atm.shape[0]
    owners = river_owner.shape[0]
    small = lax.optimization_barrier(jnp.concatenate([pair_atm, pair_land, river_owner]))
    pair_atm = small[:pair_count]
    pair_land = small[pair_count : 2 * pair_count]
    river_owner = small[2 * pair_count : 2 * pair_count + owners]
    local_rows = lax.optimization_barrier(jnp.pad(atm_fields, ((0, 0), (0, 0), (0, row_width))))
    atm_fields = local_rows[:, :, :row_width]
    extended = padded(atm_fields, ((("tile", "sub"), 1),), 1)
    grad_x = x_gradient(atm_fields)
    grad_y = (extended[:, 2:, :] - extended[:, :-2, :]) * 0.5
    stacked = jnp.concatenate([atm_fields, grad_x, grad_y], axis=2).astype(jnp.bfloat16)
    picked = stacked[:, pair_atm, :]
    weights = pair_weight.reshape(pair_count, 3 * row_width, LBLK)
    partial_value = jnp.einsum("fpk,pkl->pfl", picked, weights, preferred_element_type=jnp.float32)
    owned_sums = route_partials(partial_value, pair_land, tile_count, sub_count, tile_index)
    forcing = owned_sums.reshape(field_count, LB_DEV * LBLK)
    land_forcing = forcing.astype(jnp.bfloat16)
    moisture, runoff = soil_update(forcing, land_mask, conductance, soil_moisture)
    block_count = runoff.shape[0] // RBLK
    capacity = CAP_R
    runoff_blocks = runoff.reshape(block_count, RBLK)
    hits = (river_owner[:, None] == jnp.arange(tile_count, dtype=jnp.int32)[None, :]).astype(
        jnp.int32
    )
    ranks = jnp.sum((jnp.cumsum(hits, axis=0) - hits) * hits, axis=1)
    slot_id = river_owner * capacity + ranks
    placing = slot_id[None, :] == jnp.arange(tile_count * capacity, dtype=jnp.int32)[:, None]
    values = jnp.dot(placing.astype(jnp.float32), runoff_blocks, precision=lax.Precision.HIGHEST)
    values = values.reshape(tile_count, capacity * RBLK)
    block_ids = (tile_index * sub_count + sub_index) * block_count + jnp.arange(
        block_count, dtype=jnp.int32
    )
    numbers = jnp.sum(jnp.where(placing, block_ids[None, :] + 1, 0), axis=1) - 1
    numbers = numbers.astype(jnp.float32).reshape(tile_count, capacity)
    numbers = jnp.pad(numbers, ((0, 0), (0, RBLK - capacity)))
    packed = jnp.concatenate([values, numbers], axis=1)
    got = lax.all_to_all(packed, "tile", split_axis=0, concat_axis=0, tiled=True)
    river_runoff = got[:, : capacity * RBLK].reshape(tile_count, capacity, RBLK)[None, None]
    river_blocks = got[:, capacity * RBLK : capacity * RBLK + capacity].astype(jnp.int32)[None, None]
    return (land_forcing, moisture, river_runoff, river_blocks)


def solution(mesh):
    return jax.shard_map(
        on_device,
        mesh=mesh,
        in_specs=(
            P(None, ("tile", "sub"), None),
            P(("tile", "sub")),
            P(("tile", "sub")),
            P(("tile", "sub"), None, None, None),
            P(("tile", "sub")),
            P(None, ("tile", "sub")),
            P(None, ("tile", "sub")),
            P(("tile", "sub")),
        ),
        out_specs=(
            P(None, ("tile", "sub")),
            P(None, ("tile", "sub")),
            P("tile", "sub", None, None, None),
            P("tile", "sub", None, None),
        ),
        check_vma=False,
    )
```

```python
import jax
import jax.numpy as jnp
from jax import lax
from jax.sharding import PartitionSpec as P
from jax.experimental import pallas as pl
from jax.experimental.pallas import tpu as pltpu

SOIL_STEPS = 4
LBLK = 512
RBLK = 128
LB_DEV = 16


def passed_along(block, axis, distance):
    devices = range(lax.axis_size(axis))
    route = [((i - distance) % len(devices), i) for i in devices]
    return lax.ppermute(block, axis, route)


def padded(array, sides, width):
    for axis, dim in sides:
        devices, length = (lax.axis_size(axis), array.shape[dim])
        up = [(i, (i + 1) % devices) for i in range(devices)]
        down = [(j, i) for i, j in up]
        last = lax.slice_in_dim(array, length - width, length, axis=dim)
        initial = lax.slice_in_dim(array, 0, width, axis=dim)
        before = lax.ppermute(last, axis, up)
        after = lax.ppermute(initial, axis, down)
        array = jnp.concatenate([before, array, after], axis=dim)
    return array


def x_gradient(fields):
    inner = (fields[:, :, 2:] - fields[:, :, :-2]) * 0.5
    first = fields[:, :, 1:2] - fields[:, :, 0:1]
    last = fields[:, :, -1:] - fields[:, :, -2:-1]
    return jnp.concatenate([first, inner, last], axis=2)


def column_factors(conductance):
    layers = conductance.shape[0]
    inverse = []
    ratios = []
    for k in range(layers):
        diagonal = 1.0 + conductance[k]
        if k > 0:
            diagonal = (
                diagonal
                + conductance[k - 1]
                - conductance[k - 1] * conductance[k - 1] * inverse[k - 1]
            )
        pivot_inv = 1.0 / diagonal
        inverse.append(pivot_inv)
        ratios.append(-conductance[k] * pivot_inv)
    return (inverse, ratios)


def column_solve(moisture, source, conductance, inverse, ratios):
    layers = len(inverse)
    forward = []
    for k in range(layers):
        if k == 0:
            column_value = moisture[0] + source
        else:
            column_value = moisture[k] + conductance[k - 1] * forward[k - 1]
        forward.append(column_value * inverse[k])
    solved = [forward[layers - 1]]
    for k in range(layers - 2, -1, -1):
        solved.insert(0, forward[k] - ratios[k] * solved[0])
    return jnp.stack(solved)


def soil_kernel(
    source_ref, surface_ref, wet_ref, cond_ref, moist_ref, out_ref, runoff_ref, inv_ref, ratio_ref
):
    layers = cond_ref.shape[0]
    groups = cond_ref.shape[1] // 32

    def one_group(g, carry):
        rows = pl.ds(pl.multiple_of(g * 32, 32), 32)
        previous_cond = None
        previous_inv = None
        for k in range(layers):
            cond = cond_ref[k, rows, :]
            diagonal = 1.0 + cond
            if k > 0:
                diagonal = diagonal + previous_cond - previous_cond * previous_cond * previous_inv
            pivot_inv = 1.0 / diagonal
            inv_ref[k] = pivot_inv
            ratio_ref[k] = -cond * pivot_inv
            previous_cond = cond
            previous_inv = pivot_inv
        source = source_ref[rows, :]
        moisture = [moist_ref[k, rows, :] for k in range(layers)]
        drainage = jnp.zeros_like(source)
        for substep in range(SOIL_STEPS):
            forward = []
            for k in range(layers):
                if k == 0:
                    column_value = moisture[0] + source
                else:
                    column_value = moisture[k] + cond_ref[k - 1, rows, :] * forward[k - 1]
                forward.append(column_value * inv_ref[k])
            solved = [forward[layers - 1]]
            for k in range(layers - 2, -1, -1):
                solved.insert(0, forward[k] - ratio_ref[k] * solved[0])
            moisture = solved
            drainage = drainage + cond_ref[layers - 1, rows, :] * moisture[layers - 1]
        for k in range(layers):
            out_ref[k, rows, :] = moisture[k]
        runoff_ref[rows, :] = wet_ref[rows, :] * (SOIL_STEPS * surface_ref[rows, :] + drainage)
        return carry

    lax.fori_loop(0, groups, one_group, 0)


def soil_update(forcing, land_mask, conductance, soil_moisture):
    wetness = land_mask.astype(jnp.float32)
    source = wetness * (
        jax.nn.softplus(forcing[0]) * jax.nn.sigmoid(forcing[1])
        - 0.5 * jax.nn.sigmoid(forcing[2]) * jax.nn.softplus(forcing[3])
    )
    surface = wetness * jax.nn.softplus(forcing[0]) * (1.0 - jax.nn.sigmoid(forcing[1]))
    layers, cells = conductance.shape
    rows = cells // 128
    grid = 2
    block = rows // grid
    plane = pl.BlockSpec((block, 128), lambda i: (i, 0))
    stack = pl.BlockSpec((layers, block, 128), lambda i: (0, i, 0))
    moisture, runoff = pl.pallas_call(
        soil_kernel,
        grid=(grid,),
        in_specs=[plane, plane, plane, stack, stack],
        out_specs=[stack, plane],
        scratch_shapes=[pltpu.VMEM((layers, 32, 128), jnp.float32)] * 2,
        out_shape=[
            jax.ShapeDtypeStruct((layers, rows, 128), jnp.float32),
            jax.ShapeDtypeStruct((rows, 128), jnp.float32),
        ],
    )(
        source.reshape(rows, 128),
        surface.reshape(rows, 128),
        wetness.reshape(rows, 128),
        conductance.reshape(layers, rows, 128),
        soil_moisture.reshape(layers, rows, 128),
    )
    return (moisture.reshape(layers, cells), runoff.reshape(cells))


CAP_P = 4
CAP_R = 2


def id_rows(ids, width):
    flat = ids.reshape(-1)
    return jnp.pad(flat, (0, 8 * width - flat.shape[0])).reshape(8, width)


def route_partials(partial_value, pair_land, tile_count, sub_count, tile_index):
    pair_count, field_count, width = partial_value.shape
    owner_device = pair_land // LB_DEV
    tile_step = (owner_device // sub_count - tile_index + 1 + tile_count) % tile_count
    dest_sub = owner_device % sub_count
    group_count = 3 * sub_count
    group_id = dest_sub * 3 + tile_step
    hits = (group_id[:, None] == jnp.arange(group_count, dtype=jnp.int32)[None, :]).astype(jnp.int32)
    ranks = jnp.sum((jnp.cumsum(hits, axis=0) - hits) * hits, axis=1)
    slot_id = group_id * CAP_P + ranks
    slot_count = group_count * CAP_P
    placing = slot_id[None, :] == jnp.arange(slot_count, dtype=jnp.int32)[:, None]
    source = jnp.sum(jnp.where(placing, jnp.arange(pair_count, dtype=jnp.int32)[None, :] + 1, 0), axis=1) - 1
    filled = source >= 0
    picked = jnp.maximum(source, 0)
    rows = jnp.where(filled[:, None, None], partial_value[picked], 0.0)
    ids = jnp.where(filled, pair_land[picked] % LB_DEV, -1).astype(jnp.float32)
    chunk_rows = 3 * CAP_P * field_count
    ids = ids.reshape(sub_count, 3 * CAP_P)
    chunks = jnp.concatenate(
        [
            rows.reshape(sub_count, chunk_rows, width),
            jnp.stack([id_rows(ids[j], width) for j in range(sub_count)]),
        ],
        axis=1,
    )
    by_sub = lax.all_to_all(chunks, "sub", split_axis=0, concat_axis=0, tiled=True)
    part_rows = CAP_P * field_count
    got_ids = by_sub[:, chunk_rows, : 3 * CAP_P]
    messages = []
    for tile_step in range(3):
        data = by_sub[:, tile_step * part_rows : (tile_step + 1) * part_rows, :]
        data = data.reshape(sub_count * part_rows, width)
        step_ids = got_ids[:, tile_step * CAP_P : (tile_step + 1) * CAP_P]
        messages.append(jnp.concatenate([data, id_rows(step_ids, width)], axis=0))
    devices = range(tile_count)
    received = [
        lax.ppermute(messages[0], "tile", [(i, (i - 1) % tile_count) for i in devices]),
        messages[1],
        lax.ppermute(messages[2], "tile", [(i, (i + 1) % tile_count) for i in devices]),
    ]
    message_rows = sub_count * part_rows
    data = jnp.concatenate([m[:message_rows] for m in received], axis=0)
    slot_ids = jnp.concatenate([m[message_rows, : sub_count * CAP_P] for m in received])
    selector = (slot_ids[None, :] == jnp.arange(LB_DEV, dtype=jnp.float32)[:, None]).astype(jnp.float32)
    data = data.reshape(slot_ids.shape[0], field_count, width)
    return jnp.einsum("bs,sfl->fbl", selector, data, precision=lax.Precision.HIGHEST)


def on_device(
    atm_fields, pair_atm, pair_land, pair_weight, land_mask, conductance, soil_moisture, river_owner
):
    tile_count = lax.axis_size("tile")
    sub_count = lax.axis_size("sub")
    tile_index = lax.axis_index("tile")
    sub_index = lax.axis_index("sub")
    field_count, row_count, row_width = atm_fields.shape
    pair_count = pair_atm.shape[0]
    owners = river_owner.shape[0]
    small = lax.optimization_barrier(jnp.concatenate([pair_atm, pair_land, river_owner]))
    pair_atm = small[:pair_count]
    pair_land = small[pair_count : 2 * pair_count]
    river_owner = small[2 * pair_count : 2 * pair_count + owners]
    local_rows = lax.optimization_barrier(jnp.pad(atm_fields, ((0, 0), (0, 0), (0, row_width))))
    atm_fields = local_rows[:, :, :row_width]
    extended = padded(atm_fields, ((("tile", "sub"), 1),), 1)
    grad_x = x_gradient(atm_fields)
    grad_y = (extended[:, 2:, :] - extended[:, :-2, :]) * 0.5
    stacked = jnp.concatenate([atm_fields, grad_x, grad_y], axis=2).astype(jnp.bfloat16)
    picked = stacked[:, pair_atm, :]
    weights = pair_weight.reshape(pair_count, 3 * row_width, LBLK)
    partial_value = jnp.einsum("fpk,pkl->pfl", picked, weights, preferred_element_type=jnp.float32)
    owned_sums = route_partials(partial_value, pair_land, tile_count, sub_count, tile_index)
    forcing = owned_sums.reshape(field_count, LB_DEV * LBLK)
    land_forcing = forcing.astype(jnp.bfloat16)
    moisture, runoff = soil_update(forcing, land_mask, conductance, soil_moisture)
    block_count = runoff.shape[0] // RBLK
    capacity = CAP_R
    runoff_blocks = runoff.reshape(block_count, RBLK)
    hits = (river_owner[:, None] == jnp.arange(tile_count, dtype=jnp.int32)[None, :]).astype(
        jnp.int32
    )
    ranks = jnp.sum((jnp.cumsum(hits, axis=0) - hits) * hits, axis=1)
    slot_id = river_owner * capacity + ranks
    placing = slot_id[None, :] == jnp.arange(tile_count * capacity, dtype=jnp.int32)[:, None]
    source_block = jnp.sum(jnp.where(placing, jnp.arange(block_count, dtype=jnp.int32)[None, :] + 1, 0), axis=1) - 1
    taken = source_block >= 0
    values = jnp.where(taken[:, None], runoff_blocks[jnp.maximum(source_block, 0)], 0.0)
    values = values.reshape(tile_count, capacity, RBLK)
    block_ids = (tile_index * sub_count + sub_index) * block_count + source_block
    numbers = jnp.where(taken, block_ids, -1).astype(jnp.float32).reshape(tile_count, 1, capacity)
    numbers = jnp.pad(numbers, ((0, 0), (0, 0), (0, RBLK - capacity)))
    packed = jnp.concatenate([values, numbers], axis=1)
    got = lax.all_to_all(packed, "tile", split_axis=0, concat_axis=0, tiled=True)
    river_runoff = got[:, :capacity, :][None, None]
    river_blocks = got[:, capacity, :capacity].astype(jnp.int32)[None, None]
    return (land_forcing, moisture, river_runoff, river_blocks)


def solution(mesh):
    return jax.shard_map(
        on_device,
        mesh=mesh,
        in_specs=(
            P(None, ("tile", "sub"), None),
            P(("tile", "sub")),
            P(("tile", "sub")),
            P(("tile", "sub"), None, None, None),
            P(("tile", "sub")),
            P(None, ("tile", "sub")),
            P(None, ("tile", "sub")),
            P(("tile", "sub")),
        ),
        out_specs=(
            P(None, ("tile", "sub")),
            P(None, ("tile", "sub")),
            P("tile", "sub", None, None, None),
            P("tile", "sub", None, None),
        ),
        check_vma=False,
    )
```

```python
import jax
import jax.numpy as jnp
from jax import lax
from jax.sharding import PartitionSpec as P
from jax.experimental import pallas as pl
from jax.experimental.pallas import tpu as pltpu

SOIL_STEPS = 4
LBLK = 512
RBLK = 128
LB_DEV = 16


def passed_along(block, axis, distance):
    devices = range(lax.axis_size(axis))
    route = [((i - distance) % len(devices), i) for i in devices]
    return lax.ppermute(block, axis, route)


def padded(array, sides, width):
    for axis, dim in sides:
        devices, length = (lax.axis_size(axis), array.shape[dim])
        up = [(i, (i + 1) % devices) for i in range(devices)]
        down = [(j, i) for i, j in up]
        last = lax.slice_in_dim(array, length - width, length, axis=dim)
        initial = lax.slice_in_dim(array, 0, width, axis=dim)
        before = lax.ppermute(last, axis, up)
        after = lax.ppermute(initial, axis, down)
        array = jnp.concatenate([before, array, after], axis=dim)
    return array


def x_gradient(fields):
    inner = (fields[:, :, 2:] - fields[:, :, :-2]) * 0.5
    first = fields[:, :, 1:2] - fields[:, :, 0:1]
    last = fields[:, :, -1:] - fields[:, :, -2:-1]
    return jnp.concatenate([first, inner, last], axis=2)


def column_factors(conductance):
    layers = conductance.shape[0]
    inverse = []
    ratios = []
    for k in range(layers):
        diagonal = 1.0 + conductance[k]
        if k > 0:
            diagonal = (
                diagonal
                + conductance[k - 1]
                - conductance[k - 1] * conductance[k - 1] * inverse[k - 1]
            )
        pivot_inv = 1.0 / diagonal
        inverse.append(pivot_inv)
        ratios.append(-conductance[k] * pivot_inv)
    return (inverse, ratios)


def column_solve(moisture, source, conductance, inverse, ratios):
    layers = len(inverse)
    forward = []
    for k in range(layers):
        if k == 0:
            column_value = moisture[0] + source
        else:
            column_value = moisture[k] + conductance[k - 1] * forward[k - 1]
        forward.append(column_value * inverse[k])
    solved = [forward[layers - 1]]
    for k in range(layers - 2, -1, -1):
        solved.insert(0, forward[k] - ratios[k] * solved[0])
    return jnp.stack(solved)


def soil_kernel(
    source_ref, surface_ref, wet_ref, cond_ref, moist_ref, out_ref, runoff_ref, inv_ref, ratio_ref
):
    layers = cond_ref.shape[0]
    groups = cond_ref.shape[1] // 32

    def one_group(g, carry):
        rows = pl.ds(pl.multiple_of(g * 32, 32), 32)
        previous_cond = None
        previous_inv = None
        for k in range(layers):
            cond = cond_ref[k, rows, :]
            diagonal = 1.0 + cond
            if k > 0:
                diagonal = diagonal + previous_cond - previous_cond * previous_cond * previous_inv
            pivot_inv = 1.0 / diagonal
            inv_ref[k] = pivot_inv
            ratio_ref[k] = -cond * pivot_inv
            previous_cond = cond
            previous_inv = pivot_inv
        source = source_ref[rows, :]
        moisture = [moist_ref[k, rows, :] for k in range(layers)]
        drainage = jnp.zeros_like(source)
        for substep in range(SOIL_STEPS):
            forward = []
            for k in range(layers):
                if k == 0:
                    column_value = moisture[0] + source
                else:
                    column_value = moisture[k] + cond_ref[k - 1, rows, :] * forward[k - 1]
                forward.append(column_value * inv_ref[k])
            solved = [forward[layers - 1]]
            for k in range(layers - 2, -1, -1):
                solved.insert(0, forward[k] - ratio_ref[k] * solved[0])
            moisture = solved
            drainage = drainage + cond_ref[layers - 1, rows, :] * moisture[layers - 1]
        for k in range(layers):
            out_ref[k, rows, :] = moisture[k]
        runoff_ref[rows, :] = wet_ref[rows, :] * (SOIL_STEPS * surface_ref[rows, :] + drainage)
        return carry

    lax.fori_loop(0, groups, one_group, 0)


def soil_update(forcing, land_mask, conductance, soil_moisture):
    wetness = land_mask.astype(jnp.float32)
    source = wetness * (
        jax.nn.softplus(forcing[0]) * jax.nn.sigmoid(forcing[1])
        - 0.5 * jax.nn.sigmoid(forcing[2]) * jax.nn.softplus(forcing[3])
    )
    surface = wetness * jax.nn.softplus(forcing[0]) * (1.0 - jax.nn.sigmoid(forcing[1]))
    layers, cells = conductance.shape
    rows = cells // 128
    grid = 2
    block = rows // grid
    plane = pl.BlockSpec((block, 128), lambda i: (i, 0))
    stack = pl.BlockSpec((layers, block, 128), lambda i: (0, i, 0))
    moisture, runoff = pl.pallas_call(
        soil_kernel,
        grid=(grid,),
        in_specs=[plane, plane, plane, stack, stack],
        out_specs=[stack, plane],
        scratch_shapes=[pltpu.VMEM((layers, 32, 128), jnp.float32)] * 2,
        out_shape=[
            jax.ShapeDtypeStruct((layers, rows, 128), jnp.float32),
            jax.ShapeDtypeStruct((rows, 128), jnp.float32),
        ],
    )(
        source.reshape(rows, 128),
        surface.reshape(rows, 128),
        wetness.reshape(rows, 128),
        conductance.reshape(layers, rows, 128),
        soil_moisture.reshape(layers, rows, 128),
    )
    return (moisture.reshape(layers, cells), runoff.reshape(cells))


CAP_P = 4
CAP_R = 2


def id_rows(ids, width):
    flat = ids.reshape(-1)
    return jnp.pad(flat, (0, 8 * width - flat.shape[0])).reshape(8, width)


def route_partials(partial_value, pair_land, tile_count, sub_count, tile_index):
    pair_count, field_count, width = partial_value.shape
    owner_device = pair_land // LB_DEV
    tile_step = (owner_device // sub_count - tile_index + 1 + tile_count) % tile_count
    dest_sub = owner_device % sub_count
    group_count = 3 * sub_count
    group_id = dest_sub * 3 + tile_step
    hits = (group_id[:, None] == jnp.arange(group_count, dtype=jnp.int32)[None, :]).astype(jnp.int32)
    ranks = jnp.sum((jnp.cumsum(hits, axis=0) - hits) * hits, axis=1)
    slot_id = group_id * CAP_P + ranks
    slot_count = group_count * CAP_P
    placing = slot_id[None, :] == jnp.arange(slot_count, dtype=jnp.int32)[:, None]
    source = jnp.sum(jnp.where(placing, jnp.arange(pair_count, dtype=jnp.int32)[None, :] + 1, 0), axis=1) - 1
    filled = source >= 0
    picked = jnp.maximum(source, 0)
    rows = jnp.where(filled[:, None, None], partial_value[picked], 0.0)
    ids = jnp.where(filled, pair_land[picked] % LB_DEV, -1).astype(jnp.float32)
    chunk_rows = 3 * CAP_P * field_count
    ids = ids.reshape(sub_count, 3 * CAP_P)
    chunks = jnp.concatenate(
        [
            rows.reshape(sub_count, chunk_rows, width),
            jnp.stack([id_rows(ids[j], width) for j in range(sub_count)]),
        ],
        axis=1,
    )
    sub_index = lax.axis_index("sub")
    by_sub = [lax.dynamic_index_in_dim(chunks, sub_index, 0, keepdims=False)]
    for shift in range(1, sub_count):
        chunk = lax.dynamic_index_in_dim(chunks, (sub_index + shift) % sub_count, 0, keepdims=False)
        route = [(i, (i + shift) % sub_count) for i in range(sub_count)]
        by_sub.append(lax.ppermute(chunk, "sub", route))
    by_sub = jnp.stack(by_sub)
    part_rows = CAP_P * field_count
    got_ids = by_sub[:, chunk_rows, : 3 * CAP_P]
    messages = []
    for tile_step in range(3):
        data = by_sub[:, tile_step * part_rows : (tile_step + 1) * part_rows, :]
        data = data.reshape(sub_count * part_rows, width)
        step_ids = got_ids[:, tile_step * CAP_P : (tile_step + 1) * CAP_P]
        messages.append(jnp.concatenate([data, id_rows(step_ids, width)], axis=0))
    devices = range(tile_count)
    received = [
        lax.ppermute(messages[0], "tile", [(i, (i - 1) % tile_count) for i in devices]),
        messages[1],
        lax.ppermute(messages[2], "tile", [(i, (i + 1) % tile_count) for i in devices]),
    ]
    message_rows = sub_count * part_rows
    data = jnp.concatenate([m[:message_rows] for m in received], axis=0)
    slot_ids = jnp.concatenate([m[message_rows, : sub_count * CAP_P] for m in received])
    selector = (slot_ids[None, :] == jnp.arange(LB_DEV, dtype=jnp.float32)[:, None]).astype(jnp.float32)
    data = data.reshape(slot_ids.shape[0], field_count, width)
    return jnp.einsum("bs,sfl->fbl", selector, data, precision=lax.Precision.HIGHEST)


def on_device(
    atm_fields, pair_atm, pair_land, pair_weight, land_mask, conductance, soil_moisture, river_owner
):
    tile_count = lax.axis_size("tile")
    sub_count = lax.axis_size("sub")
    tile_index = lax.axis_index("tile")
    sub_index = lax.axis_index("sub")
    field_count, row_count, row_width = atm_fields.shape
    pair_count = pair_atm.shape[0]
    owners = river_owner.shape[0]
    small = lax.optimization_barrier(jnp.concatenate([pair_atm, pair_land, river_owner]))
    pair_atm = small[:pair_count]
    pair_land = small[pair_count : 2 * pair_count]
    river_owner = small[2 * pair_count : 2 * pair_count + owners]
    local_rows = lax.optimization_barrier(jnp.pad(atm_fields, ((0, 0), (0, 0), (0, row_width))))
    atm_fields = local_rows[:, :, :row_width]
    extended = padded(atm_fields, ((("tile", "sub"), 1),), 1)
    grad_x = x_gradient(atm_fields)
    grad_y = (extended[:, 2:, :] - extended[:, :-2, :]) * 0.5
    stacked = jnp.concatenate([atm_fields, grad_x, grad_y], axis=2).astype(jnp.bfloat16)
    picked = stacked[:, pair_atm, :]
    weights = pair_weight.reshape(pair_count, 3 * row_width, LBLK)
    partial_value = jnp.einsum("fpk,pkl->pfl", picked, weights, preferred_element_type=jnp.float32)
    owned_sums = route_partials(partial_value, pair_land, tile_count, sub_count, tile_index)
    forcing = owned_sums.reshape(field_count, LB_DEV * LBLK)
    land_forcing = forcing.astype(jnp.bfloat16)
    moisture, runoff = soil_update(forcing, land_mask, conductance, soil_moisture)
    block_count = runoff.shape[0] // RBLK
    capacity = CAP_R
    runoff_blocks = runoff.reshape(block_count, RBLK)
    hits = (river_owner[:, None] == jnp.arange(tile_count, dtype=jnp.int32)[None, :]).astype(
        jnp.int32
    )
    ranks = jnp.sum((jnp.cumsum(hits, axis=0) - hits) * hits, axis=1)
    slot_id = river_owner * capacity + ranks
    placing = slot_id[None, :] == jnp.arange(tile_count * capacity, dtype=jnp.int32)[:, None]
    values = jnp.dot(placing.astype(jnp.float32), runoff_blocks, precision=lax.Precision.HIGHEST)
    values = values.reshape(tile_count, capacity * RBLK)
    block_ids = (tile_index * sub_count + sub_index) * block_count + jnp.arange(
        block_count, dtype=jnp.int32
    )
    numbers = jnp.sum(jnp.where(placing, block_ids[None, :] + 1, 0), axis=1) - 1
    numbers = numbers.astype(jnp.float32).reshape(tile_count, capacity)
    numbers = jnp.pad(numbers, ((0, 0), (0, RBLK - capacity)))
    packed = jnp.concatenate([values, numbers], axis=1)
    got = lax.all_to_all(packed, "tile", split_axis=0, concat_axis=0, tiled=True)
    river_runoff = got[:, : capacity * RBLK].reshape(tile_count, capacity, RBLK)[None, None]
    river_blocks = got[:, capacity * RBLK : capacity * RBLK + capacity].astype(jnp.int32)[None, None]
    return (land_forcing, moisture, river_runoff, river_blocks)


def solution(mesh):
    return jax.shard_map(
        on_device,
        mesh=mesh,
        in_specs=(
            P(None, ("tile", "sub"), None),
            P(("tile", "sub")),
            P(("tile", "sub")),
            P(("tile", "sub"), None, None, None),
            P(("tile", "sub")),
            P(None, ("tile", "sub")),
            P(None, ("tile", "sub")),
            P(("tile", "sub")),
        ),
        out_specs=(
            P(None, ("tile", "sub")),
            P(None, ("tile", "sub")),
            P("tile", "sub", None, None, None),
            P("tile", "sub", None, None),
        ),
        check_vma=False,
    )
```

```python
import jax
import jax.numpy as jnp
from jax import lax
from jax.sharding import PartitionSpec as P
from jax.experimental import pallas as pl
from jax.experimental.pallas import tpu as pltpu

SOIL_STEPS = 4
LBLK = 512
RBLK = 128
LB_DEV = 16


def passed_along(block, axis, distance):
    devices = range(lax.axis_size(axis))
    route = [((i - distance) % len(devices), i) for i in devices]
    return lax.ppermute(block, axis, route)


def padded(array, sides, width):
    for axis, dim in sides:
        devices, length = (lax.axis_size(axis), array.shape[dim])
        up = [(i, (i + 1) % devices) for i in range(devices)]
        down = [(j, i) for i, j in up]
        last = lax.slice_in_dim(array, length - width, length, axis=dim)
        initial = lax.slice_in_dim(array, 0, width, axis=dim)
        before = lax.ppermute(last, axis, up)
        after = lax.ppermute(initial, axis, down)
        array = jnp.concatenate([before, array, after], axis=dim)
    return array


def x_gradient(fields):
    inner = (fields[:, :, 2:] - fields[:, :, :-2]) * 0.5
    first = fields[:, :, 1:2] - fields[:, :, 0:1]
    last = fields[:, :, -1:] - fields[:, :, -2:-1]
    return jnp.concatenate([first, inner, last], axis=2)


def column_factors(conductance):
    layers = conductance.shape[0]
    inverse = []
    ratios = []
    for k in range(layers):
        diagonal = 1.0 + conductance[k]
        if k > 0:
            diagonal = (
                diagonal
                + conductance[k - 1]
                - conductance[k - 1] * conductance[k - 1] * inverse[k - 1]
            )
        pivot_inv = 1.0 / diagonal
        inverse.append(pivot_inv)
        ratios.append(-conductance[k] * pivot_inv)
    return (inverse, ratios)


def column_solve(moisture, source, conductance, inverse, ratios):
    layers = len(inverse)
    forward = []
    for k in range(layers):
        if k == 0:
            column_value = moisture[0] + source
        else:
            column_value = moisture[k] + conductance[k - 1] * forward[k - 1]
        forward.append(column_value * inverse[k])
    solved = [forward[layers - 1]]
    for k in range(layers - 2, -1, -1):
        solved.insert(0, forward[k] - ratios[k] * solved[0])
    return jnp.stack(solved)


def response_kernel(
    cond_ref, moist_ref, base_ref, unit_ref, base_drain_ref, unit_drain_ref, inv_ref, ratio_ref
):
    layers = cond_ref.shape[0]
    rows = pl.ds(0, cond_ref.shape[1])
    previous_cond = None
    previous_inv = None
    for k in range(layers):
        cond = cond_ref[k, rows, :]
        diagonal = 1.0 + cond
        if k > 0:
            diagonal = diagonal + previous_cond - previous_cond * previous_cond * previous_inv
        pivot_inv = 1.0 / diagonal
        inv_ref[k] = pivot_inv
        ratio_ref[k] = -cond * pivot_inv
        previous_cond = cond
        previous_inv = pivot_inv

    def solve(moisture, source):
        drainage = None
        for substep in range(SOIL_STEPS):
            forward = []
            for k in range(layers):
                if k == 0:
                    column_value = moisture[0] if source is None else moisture[0] + source
                else:
                    column_value = moisture[k] + cond_ref[k - 1, rows, :] * forward[k - 1]
                forward.append(column_value * inv_ref[k])
            solved = [forward[layers - 1]]
            for k in range(layers - 2, -1, -1):
                solved.insert(0, forward[k] - ratio_ref[k] * solved[0])
            moisture = solved
            drained = cond_ref[layers - 1, rows, :] * moisture[layers - 1]
            drainage = drained if drainage is None else drainage + drained
        return (moisture, drainage)

    base, base_drain = solve([moist_ref[k, rows, :] for k in range(layers)], None)
    for k in range(layers):
        base_ref[k, rows, :] = base[k]
    base_drain_ref[rows, :] = base_drain
    zero = jnp.zeros_like(base_drain)
    unit, unit_drain = solve([zero] * layers, zero + 1.0)
    for k in range(layers):
        unit_ref[k, rows, :] = unit[k]
    unit_drain_ref[rows, :] = unit_drain


def soil_response(conductance, soil_moisture):
    layers, rows, lanes = conductance.shape
    grid = 2
    block = rows // grid
    plane = pl.BlockSpec((block, lanes), lambda i: (i, 0))
    stack = pl.BlockSpec((layers, block, lanes), lambda i: (0, i, 0))
    layer_shape = jax.ShapeDtypeStruct((layers, rows, lanes), jnp.float32)
    plane_shape = jax.ShapeDtypeStruct((rows, lanes), jnp.float32)
    return pl.pallas_call(
        response_kernel,
        grid=(grid,),
        in_specs=[stack, stack],
        out_specs=[stack, stack, plane, plane],
        scratch_shapes=[pltpu.VMEM((layers, block, lanes), jnp.float32)] * 2,
        out_shape=[layer_shape, layer_shape, plane_shape, plane_shape],
    )(conductance, soil_moisture)


def soil_update(source, surface, wetness, response):
    base, unit, base_drain, unit_drain = response
    layers, rows, lanes = base.shape
    source = source.reshape(rows, lanes)
    moisture = base + source[None] * unit
    runoff = wetness * (SOIL_STEPS * surface.reshape(rows, lanes) + (base_drain + source * unit_drain))
    return (moisture.reshape(layers, rows * lanes), runoff.reshape(rows * lanes))


CAP_P = 4
CAP_R = 2


def id_rows(ids, width):
    flat = ids.reshape(-1)
    return jnp.pad(flat, (0, 8 * width - flat.shape[0])).reshape(8, width)


def route_partials(partial_value, pair_land, tile_count, sub_count, tile_index):
    pair_count, field_count, width = partial_value.shape
    owner_device = pair_land // LB_DEV
    tile_step = (owner_device // sub_count - tile_index + 1 + tile_count) % tile_count
    dest_sub = owner_device % sub_count
    group_count = 3 * sub_count
    group_id = dest_sub * 3 + tile_step
    hits = (group_id[:, None] == jnp.arange(group_count, dtype=jnp.int32)[None, :]).astype(jnp.int32)
    ranks = jnp.sum((jnp.cumsum(hits, axis=0) - hits) * hits, axis=1)
    slot_id = group_id * CAP_P + ranks
    slot_count = group_count * CAP_P
    placing = slot_id[None, :] == jnp.arange(slot_count, dtype=jnp.int32)[:, None]
    source = jnp.sum(jnp.where(placing, jnp.arange(pair_count, dtype=jnp.int32)[None, :] + 1, 0), axis=1) - 1
    filled = source >= 0
    picked = jnp.maximum(source, 0)
    rows = jnp.where(filled[:, None, None], partial_value[picked], 0.0)
    ids = jnp.where(filled, pair_land[picked] % LB_DEV, -1).astype(jnp.float32)
    chunk_rows = 3 * CAP_P * field_count
    ids = ids.reshape(sub_count, 3 * CAP_P)
    chunks = jnp.concatenate(
        [
            rows.reshape(sub_count, chunk_rows, width),
            jnp.stack([id_rows(ids[j], width) for j in range(sub_count)]),
        ],
        axis=1,
    )
    by_sub = lax.all_to_all(chunks, "sub", split_axis=0, concat_axis=0, tiled=True)
    part_rows = CAP_P * field_count
    got_ids = by_sub[:, chunk_rows, : 3 * CAP_P]
    messages = []
    for tile_step in range(3):
        data = by_sub[:, tile_step * part_rows : (tile_step + 1) * part_rows, :]
        data = data.reshape(sub_count * part_rows, width)
        step_ids = got_ids[:, tile_step * CAP_P : (tile_step + 1) * CAP_P]
        messages.append(jnp.concatenate([data, id_rows(step_ids, width)], axis=0))
    devices = range(tile_count)
    received = [
        lax.ppermute(messages[0], "tile", [(i, (i - 1) % tile_count) for i in devices]),
        messages[1],
        lax.ppermute(messages[2], "tile", [(i, (i + 1) % tile_count) for i in devices]),
    ]
    message_rows = sub_count * part_rows
    data = jnp.concatenate([m[:message_rows] for m in received], axis=0)
    slot_ids = jnp.concatenate([m[message_rows, : sub_count * CAP_P] for m in received])
    selector = (slot_ids[None, :] == jnp.arange(LB_DEV, dtype=jnp.float32)[:, None]).astype(jnp.float32)
    data = data.reshape(slot_ids.shape[0], field_count, width)
    return jnp.einsum("bs,sfl->fbl", selector, data, precision=lax.Precision.HIGHEST)


def on_device(
    atm_fields, pair_atm, pair_land, pair_weight, land_mask, conductance, soil_moisture, river_owner
):
    tile_count = lax.axis_size("tile")
    sub_count = lax.axis_size("sub")
    tile_index = lax.axis_index("tile")
    sub_index = lax.axis_index("sub")
    field_count, row_count, row_width = atm_fields.shape
    pair_count = pair_atm.shape[0]
    owners = river_owner.shape[0]
    small = lax.optimization_barrier(jnp.concatenate([pair_atm, pair_land, river_owner]))
    pair_atm = small[:pair_count]
    pair_land = small[pair_count : 2 * pair_count]
    river_owner = small[2 * pair_count : 2 * pair_count + owners]
    local_rows = lax.optimization_barrier(jnp.pad(atm_fields, ((0, 0), (0, 0), (0, row_width))))
    atm_fields = local_rows[:, :, :row_width]
    extended = padded(atm_fields, ((("tile", "sub"), 1),), 1)
    grad_x = x_gradient(atm_fields)
    grad_y = (extended[:, 2:, :] - extended[:, :-2, :]) * 0.5
    stacked = jnp.concatenate([atm_fields, grad_x, grad_y], axis=2).astype(jnp.bfloat16)
    picked = stacked[:, pair_atm, :]
    weights = pair_weight.reshape(pair_count, 3 * row_width, LBLK)
    partial_value = jnp.einsum("fpk,pkl->pfl", picked, weights, preferred_element_type=jnp.float32)
    owned_sums = route_partials(partial_value, pair_land, tile_count, sub_count, tile_index)
    forcing = owned_sums.reshape(field_count, LB_DEV * LBLK)
    land_forcing = forcing.astype(jnp.bfloat16)
    layers, cell_count = conductance.shape
    tiles = (cell_count // RBLK, RBLK)
    response = soil_response(
        conductance.reshape((layers,) + tiles), soil_moisture.reshape((layers,) + tiles)
    )
    wetness = land_mask.astype(jnp.float32)
    source = wetness * (
        jax.nn.softplus(forcing[0]) * jax.nn.sigmoid(forcing[1])
        - 0.5 * jax.nn.sigmoid(forcing[2]) * jax.nn.softplus(forcing[3])
    )
    surface = wetness * jax.nn.softplus(forcing[0]) * (1.0 - jax.nn.sigmoid(forcing[1]))
    moisture, runoff = soil_update(source, surface, wetness.reshape(tiles), response)
    block_count = runoff.shape[0] // RBLK
    capacity = CAP_R
    runoff_blocks = runoff.reshape(block_count, RBLK)
    hits = (river_owner[:, None] == jnp.arange(tile_count, dtype=jnp.int32)[None, :]).astype(
        jnp.int32
    )
    ranks = jnp.sum((jnp.cumsum(hits, axis=0) - hits) * hits, axis=1)
    slot_id = river_owner * capacity + ranks
    placing = slot_id[None, :] == jnp.arange(tile_count * capacity, dtype=jnp.int32)[:, None]
    values = jnp.dot(placing.astype(jnp.float32), runoff_blocks, precision=lax.Precision.HIGHEST)
    values = values.reshape(tile_count, capacity * RBLK)
    block_ids = (tile_index * sub_count + sub_index) * block_count + jnp.arange(
        block_count, dtype=jnp.int32
    )
    numbers = jnp.sum(jnp.where(placing, block_ids[None, :] + 1, 0), axis=1) - 1
    numbers = numbers.astype(jnp.float32).reshape(tile_count, capacity)
    numbers = jnp.pad(numbers, ((0, 0), (0, RBLK - capacity)))
    packed = jnp.concatenate([values, numbers], axis=1)
    got = lax.all_to_all(packed, "tile", split_axis=0, concat_axis=0, tiled=True)
    river_runoff = got[:, : capacity * RBLK].reshape(tile_count, capacity, RBLK)[None, None]
    river_blocks = got[:, capacity * RBLK : capacity * RBLK + capacity].astype(jnp.int32)[None, None]
    return (land_forcing, moisture, river_runoff, river_blocks)


def solution(mesh):
    return jax.shard_map(
        on_device,
        mesh=mesh,
        in_specs=(
            P(None, ("tile", "sub"), None),
            P(("tile", "sub")),
            P(("tile", "sub")),
            P(("tile", "sub"), None, None, None),
            P(("tile", "sub")),
            P(None, ("tile", "sub")),
            P(None, ("tile", "sub")),
            P(("tile", "sub")),
        ),
        out_specs=(
            P(None, ("tile", "sub")),
            P(None, ("tile", "sub")),
            P("tile", "sub", None, None, None),
            P("tile", "sub", None, None),
        ),
        check_vma=False,
    )
```

```python
import jax
import jax.numpy as jnp
from jax import lax
from jax.sharding import PartitionSpec as P
from jax.experimental import pallas as pl
from jax.experimental.pallas import tpu as pltpu

SOIL_STEPS = 4
LBLK = 512
RBLK = 128
LB_DEV = 16


def passed_along(block, axis, distance):
    devices = range(lax.axis_size(axis))
    route = [((i - distance) % len(devices), i) for i in devices]
    return lax.ppermute(block, axis, route)


def padded(array, sides, width):
    for axis, dim in sides:
        devices, length = (lax.axis_size(axis), array.shape[dim])
        up = [(i, (i + 1) % devices) for i in range(devices)]
        down = [(j, i) for i, j in up]
        last = lax.slice_in_dim(array, length - width, length, axis=dim)
        initial = lax.slice_in_dim(array, 0, width, axis=dim)
        before = lax.ppermute(last, axis, up)
        after = lax.ppermute(initial, axis, down)
        array = jnp.concatenate([before, array, after], axis=dim)
    return array


def x_gradient(fields):
    inner = (fields[:, :, 2:] - fields[:, :, :-2]) * 0.5
    first = fields[:, :, 1:2] - fields[:, :, 0:1]
    last = fields[:, :, -1:] - fields[:, :, -2:-1]
    return jnp.concatenate([first, inner, last], axis=2)


def column_factors(conductance):
    layers = conductance.shape[0]
    inverse = []
    ratios = []
    for k in range(layers):
        diagonal = 1.0 + conductance[k]
        if k > 0:
            diagonal = (
                diagonal
                + conductance[k - 1]
                - conductance[k - 1] * conductance[k - 1] * inverse[k - 1]
            )
        pivot_inv = 1.0 / diagonal
        inverse.append(pivot_inv)
        ratios.append(-conductance[k] * pivot_inv)
    return (inverse, ratios)


def column_solve(moisture, source, conductance, inverse, ratios):
    layers = len(inverse)
    forward = []
    for k in range(layers):
        if k == 0:
            column_value = moisture[0] + source
        else:
            column_value = moisture[k] + conductance[k - 1] * forward[k - 1]
        forward.append(column_value * inverse[k])
    solved = [forward[layers - 1]]
    for k in range(layers - 2, -1, -1):
        solved.insert(0, forward[k] - ratios[k] * solved[0])
    return jnp.stack(solved)


def response_kernel(
    cond_ref, moist_ref, base_ref, unit_ref, base_drain_ref, unit_drain_ref, inv_ref, ratio_ref
):
    layers = cond_ref.shape[0]
    rows = pl.ds(0, cond_ref.shape[1])
    previous_cond = None
    previous_inv = None
    for k in range(layers):
        cond = cond_ref[k, rows, :]
        diagonal = 1.0 + cond
        if k > 0:
            diagonal = diagonal + previous_cond - previous_cond * previous_cond * previous_inv
        pivot_inv = 1.0 / diagonal
        inv_ref[k] = pivot_inv
        ratio_ref[k] = -cond * pivot_inv
        previous_cond = cond
        previous_inv = pivot_inv

    def solve(moisture, source):
        drainage = None
        for substep in range(SOIL_STEPS):
            forward = []
            for k in range(layers):
                if k == 0:
                    column_value = moisture[0] if source is None else moisture[0] + source
                else:
                    column_value = moisture[k] + cond_ref[k - 1, rows, :] * forward[k - 1]
                forward.append(column_value * inv_ref[k])
            solved = [forward[layers - 1]]
            for k in range(layers - 2, -1, -1):
                solved.insert(0, forward[k] - ratio_ref[k] * solved[0])
            moisture = solved
            drained = cond_ref[layers - 1, rows, :] * moisture[layers - 1]
            drainage = drained if drainage is None else drainage + drained
        return (moisture, drainage)

    base, base_drain = solve([moist_ref[k, rows, :] for k in range(layers)], None)
    for k in range(layers):
        base_ref[k, rows, :] = base[k]
    base_drain_ref[rows, :] = base_drain
    zero = jnp.zeros_like(base_drain)
    unit, unit_drain = solve([zero] * layers, zero + 1.0)
    for k in range(layers):
        unit_ref[k, rows, :] = unit[k]
    unit_drain_ref[rows, :] = unit_drain


def soil_response(conductance, soil_moisture):
    layers, rows, lanes = conductance.shape
    grid = 2
    block = rows // grid
    plane = pl.BlockSpec((block, lanes), lambda i: (i, 0))
    stack = pl.BlockSpec((layers, block, lanes), lambda i: (0, i, 0))
    layer_shape = jax.ShapeDtypeStruct((layers, rows, lanes), jnp.float32)
    plane_shape = jax.ShapeDtypeStruct((rows, lanes), jnp.float32)
    return pl.pallas_call(
        response_kernel,
        grid=(grid,),
        in_specs=[stack, stack],
        out_specs=[stack, stack, plane, plane],
        scratch_shapes=[pltpu.VMEM((layers, block, lanes), jnp.float32)] * 2,
        out_shape=[layer_shape, layer_shape, plane_shape, plane_shape],
    )(conductance, soil_moisture)


def soil_update(source, surface, wetness, response):
    base, unit, base_drain, unit_drain = response
    layers, rows, lanes = base.shape
    source = source.reshape(rows, lanes)
    moisture = base + source[None] * unit
    runoff = wetness * (SOIL_STEPS * surface.reshape(rows, lanes) + (base_drain + source * unit_drain))
    return (moisture.reshape(layers, rows * lanes), runoff.reshape(rows * lanes))


CAP_P = 4
CAP_R = 2


def id_rows(ids, width):
    flat = ids.reshape(-1)
    return jnp.pad(flat, (0, 8 * width - flat.shape[0])).reshape(8, width)


def route_partials(partial_value, pair_land, tile_count, sub_count, tile_index):
    pair_count, field_count, width = partial_value.shape
    owner_device = pair_land // LB_DEV
    tile_step = (owner_device // sub_count - tile_index + 1 + tile_count) % tile_count
    dest_sub = owner_device % sub_count
    group_count = 3 * sub_count
    group_id = dest_sub * 3 + tile_step
    hits = (group_id[:, None] == jnp.arange(group_count, dtype=jnp.int32)[None, :]).astype(jnp.int32)
    ranks = jnp.sum((jnp.cumsum(hits, axis=0) - hits) * hits, axis=1)
    slot_id = group_id * CAP_P + ranks
    slot_count = group_count * CAP_P
    placing = slot_id[None, :] == jnp.arange(slot_count, dtype=jnp.int32)[:, None]
    source = jnp.sum(jnp.where(placing, jnp.arange(pair_count, dtype=jnp.int32)[None, :] + 1, 0), axis=1) - 1
    filled = source >= 0
    picked = jnp.maximum(source, 0)
    rows = jnp.where(filled[:, None, None], partial_value[picked], 0.0)
    ids = jnp.where(filled, pair_land[picked] % LB_DEV, -1).astype(jnp.float32)
    chunk_rows = 3 * CAP_P * field_count
    ids = ids.reshape(sub_count, 3 * CAP_P)
    chunks = jnp.concatenate(
        [
            rows.reshape(sub_count, chunk_rows, width),
            jnp.stack([id_rows(ids[j], width) for j in range(sub_count)]),
        ],
        axis=1,
    )
    by_sub = lax.all_to_all(chunks, "sub", split_axis=0, concat_axis=0, tiled=True)
    part_rows = CAP_P * field_count
    got_ids = by_sub[:, chunk_rows, : 3 * CAP_P]
    messages = []
    for tile_step in range(3):
        data = by_sub[:, tile_step * part_rows : (tile_step + 1) * part_rows, :]
        data = data.reshape(sub_count * part_rows, width)
        step_ids = got_ids[:, tile_step * CAP_P : (tile_step + 1) * CAP_P]
        messages.append(jnp.concatenate([data, id_rows(step_ids, width)], axis=0))
    devices = range(tile_count)
    received = [
        lax.ppermute(messages[0], "tile", [(i, (i - 1) % tile_count) for i in devices]),
        messages[1],
        lax.ppermute(messages[2], "tile", [(i, (i + 1) % tile_count) for i in devices]),
    ]
    message_rows = sub_count * part_rows
    data = jnp.concatenate([m[:message_rows] for m in received], axis=0)
    slot_ids = jnp.concatenate([m[message_rows, : sub_count * CAP_P] for m in received])
    selector = (slot_ids[None, :] == jnp.arange(LB_DEV, dtype=jnp.float32)[:, None]).astype(jnp.float32)
    data = data.reshape(slot_ids.shape[0], field_count, width)
    return jnp.einsum("bs,sfl->fbl", selector, data, precision=lax.Precision.HIGHEST)


def on_device(
    atm_fields, pair_atm, pair_land, pair_weight, land_mask, conductance, soil_moisture, river_owner
):
    tile_count = lax.axis_size("tile")
    sub_count = lax.axis_size("sub")
    tile_index = lax.axis_index("tile")
    sub_index = lax.axis_index("sub")
    field_count, row_count, row_width = atm_fields.shape
    pair_count = pair_atm.shape[0]
    owners = river_owner.shape[0]
    small = lax.optimization_barrier(jnp.concatenate([pair_atm, pair_land, river_owner]))
    pair_atm = small[:pair_count]
    pair_land = small[pair_count : 2 * pair_count]
    river_owner = small[2 * pair_count : 2 * pair_count + owners]
    devices = tile_count * sub_count
    up = [(i, (i + 1) % devices) for i in range(devices)]
    down = [(j, i) for i, j in up]
    before = lax.ppermute(atm_fields[:, row_count - 1 :, :], ("tile", "sub"), up)
    local_rows = lax.optimization_barrier(jnp.pad(atm_fields, ((0, 0), (0, 0), (0, row_width))))
    atm_fields = local_rows[:, :, :row_width]
    after = lax.ppermute(atm_fields[:, :1, :], ("tile", "sub"), down)
    extended = jnp.concatenate([before, atm_fields, after], axis=1)
    grad_x = x_gradient(atm_fields)
    grad_y = (extended[:, 2:, :] - extended[:, :-2, :]) * 0.5
    stacked = jnp.concatenate([atm_fields, grad_x, grad_y], axis=2).astype(jnp.bfloat16)
    picked = stacked[:, pair_atm, :]
    weights = pair_weight.reshape(pair_count, 3 * row_width, LBLK)
    partial_value = jnp.einsum("fpk,pkl->pfl", picked, weights, preferred_element_type=jnp.float32)
    owned_sums = route_partials(partial_value, pair_land, tile_count, sub_count, tile_index)
    forcing = owned_sums.reshape(field_count, LB_DEV * LBLK)
    land_forcing = forcing.astype(jnp.bfloat16)
    layers, cell_count = conductance.shape
    tiles = (cell_count // RBLK, RBLK)
    response = soil_response(
        conductance.reshape((layers,) + tiles), soil_moisture.reshape((layers,) + tiles)
    )
    wetness = land_mask.astype(jnp.float32)
    source = wetness * (
        jax.nn.softplus(forcing[0]) * jax.nn.sigmoid(forcing[1])
        - 0.5 * jax.nn.sigmoid(forcing[2]) * jax.nn.softplus(forcing[3])
    )
    surface = wetness * jax.nn.softplus(forcing[0]) * (1.0 - jax.nn.sigmoid(forcing[1]))
    moisture, runoff = soil_update(source, surface, wetness.reshape(tiles), response)
    block_count = runoff.shape[0] // RBLK
    capacity = CAP_R
    runoff_blocks = runoff.reshape(block_count, RBLK)
    hits = (river_owner[:, None] == jnp.arange(tile_count, dtype=jnp.int32)[None, :]).astype(
        jnp.int32
    )
    ranks = jnp.sum((jnp.cumsum(hits, axis=0) - hits) * hits, axis=1)
    slot_id = river_owner * capacity + ranks
    placing = slot_id[None, :] == jnp.arange(tile_count * capacity, dtype=jnp.int32)[:, None]
    values = jnp.dot(placing.astype(jnp.float32), runoff_blocks, precision=lax.Precision.HIGHEST)
    values = values.reshape(tile_count, capacity * RBLK)
    block_ids = (tile_index * sub_count + sub_index) * block_count + jnp.arange(
        block_count, dtype=jnp.int32
    )
    numbers = jnp.sum(jnp.where(placing, block_ids[None, :] + 1, 0), axis=1) - 1
    numbers = numbers.astype(jnp.float32).reshape(tile_count, capacity)
    numbers = jnp.pad(numbers, ((0, 0), (0, RBLK - capacity)))
    packed = jnp.concatenate([values, numbers], axis=1)
    got = lax.all_to_all(packed, "tile", split_axis=0, concat_axis=0, tiled=True)
    river_runoff = got[:, : capacity * RBLK].reshape(tile_count, capacity, RBLK)[None, None]
    river_blocks = got[:, capacity * RBLK : capacity * RBLK + capacity].astype(jnp.int32)[None, None]
    return (land_forcing, moisture, river_runoff, river_blocks)


def solution(mesh):
    return jax.shard_map(
        on_device,
        mesh=mesh,
        in_specs=(
            P(None, ("tile", "sub"), None),
            P(("tile", "sub")),
            P(("tile", "sub")),
            P(("tile", "sub"), None, None, None),
            P(("tile", "sub")),
            P(None, ("tile", "sub")),
            P(None, ("tile", "sub")),
            P(("tile", "sub")),
        ),
        out_specs=(
            P(None, ("tile", "sub")),
            P(None, ("tile", "sub")),
            P("tile", "sub", None, None, None),
            P("tile", "sub", None, None),
        ),
        check_vma=False,
    )
```

```python
import jax
import jax.numpy as jnp
from jax import lax
from jax.sharding import PartitionSpec as P
from jax.experimental import pallas as pl
from jax.experimental.pallas import tpu as pltpu

SOIL_STEPS = 4
LBLK = 512
RBLK = 128
LB_DEV = 16


def passed_along(block, axis, distance):
    devices = range(lax.axis_size(axis))
    route = [((i - distance) % len(devices), i) for i in devices]
    return lax.ppermute(block, axis, route)


def padded(array, sides, width):
    for axis, dim in sides:
        devices, length = (lax.axis_size(axis), array.shape[dim])
        up = [(i, (i + 1) % devices) for i in range(devices)]
        down = [(j, i) for i, j in up]
        last = lax.slice_in_dim(array, length - width, length, axis=dim)
        initial = lax.slice_in_dim(array, 0, width, axis=dim)
        before = lax.ppermute(last, axis, up)
        after = lax.ppermute(initial, axis, down)
        array = jnp.concatenate([before, array, after], axis=dim)
    return array


def x_gradient(fields):
    inner = (fields[:, :, 2:] - fields[:, :, :-2]) * 0.5
    first = fields[:, :, 1:2] - fields[:, :, 0:1]
    last = fields[:, :, -1:] - fields[:, :, -2:-1]
    return jnp.concatenate([first, inner, last], axis=2)


def column_factors(conductance):
    layers = conductance.shape[0]
    inverse = []
    ratios = []
    for k in range(layers):
        diagonal = 1.0 + conductance[k]
        if k > 0:
            diagonal = (
                diagonal
                + conductance[k - 1]
                - conductance[k - 1] * conductance[k - 1] * inverse[k - 1]
            )
        pivot_inv = 1.0 / diagonal
        inverse.append(pivot_inv)
        ratios.append(-conductance[k] * pivot_inv)
    return (inverse, ratios)


def column_solve(moisture, source, conductance, inverse, ratios):
    layers = len(inverse)
    forward = []
    for k in range(layers):
        if k == 0:
            column_value = moisture[0] + source
        else:
            column_value = moisture[k] + conductance[k - 1] * forward[k - 1]
        forward.append(column_value * inverse[k])
    solved = [forward[layers - 1]]
    for k in range(layers - 2, -1, -1):
        solved.insert(0, forward[k] - ratios[k] * solved[0])
    return jnp.stack(solved)


def response_kernel(
    cond_ref, moist_ref, base_ref, unit_ref, base_drain_ref, unit_drain_ref, inv_ref, ratio_ref
):
    layers = cond_ref.shape[0]
    rows = pl.ds(0, cond_ref.shape[1])
    previous_cond = None
    previous_inv = None
    for k in range(layers):
        cond = cond_ref[k, rows, :]
        diagonal = 1.0 + cond
        if k > 0:
            diagonal = diagonal + previous_cond - previous_cond * previous_cond * previous_inv
        pivot_inv = 1.0 / diagonal
        inv_ref[k] = pivot_inv
        ratio_ref[k] = -cond * pivot_inv
        previous_cond = cond
        previous_inv = pivot_inv

    def solve(moisture, source):
        drainage = None
        for substep in range(SOIL_STEPS):
            forward = []
            for k in range(layers):
                if k == 0:
                    column_value = moisture[0] if source is None else moisture[0] + source
                else:
                    column_value = moisture[k] + cond_ref[k - 1, rows, :] * forward[k - 1]
                forward.append(column_value * inv_ref[k])
            solved = [forward[layers - 1]]
            for k in range(layers - 2, -1, -1):
                solved.insert(0, forward[k] - ratio_ref[k] * solved[0])
            moisture = solved
            drained = cond_ref[layers - 1, rows, :] * moisture[layers - 1]
            drainage = drained if drainage is None else drainage + drained
        return (moisture, drainage)

    base, base_drain = solve([moist_ref[k, rows, :] for k in range(layers)], None)
    for k in range(layers):
        base_ref[k, rows, :] = base[k]
    base_drain_ref[rows, :] = base_drain
    zero = jnp.zeros_like(base_drain)
    unit, unit_drain = solve([zero] * layers, zero + 1.0)
    for k in range(layers):
        unit_ref[k, rows, :] = unit[k]
    unit_drain_ref[rows, :] = unit_drain


def soil_response(conductance, soil_moisture):
    layers, rows, lanes = conductance.shape
    grid = 2
    block = rows // grid
    plane = pl.BlockSpec((block, lanes), lambda i: (i, 0))
    stack = pl.BlockSpec((layers, block, lanes), lambda i: (0, i, 0))
    layer_shape = jax.ShapeDtypeStruct((layers, rows, lanes), jnp.float32)
    plane_shape = jax.ShapeDtypeStruct((rows, lanes), jnp.float32)
    return pl.pallas_call(
        response_kernel,
        grid=(grid,),
        in_specs=[stack, stack],
        out_specs=[stack, stack, plane, plane],
        scratch_shapes=[pltpu.VMEM((layers, block, lanes), jnp.float32)] * 2,
        out_shape=[layer_shape, layer_shape, plane_shape, plane_shape],
    )(conductance, soil_moisture)


def soil_update(source, surface, wetness, response):
    base, unit, base_drain, unit_drain = response
    layers, rows, lanes = base.shape
    source = source.reshape(rows, lanes)
    moisture = base + source[None] * unit
    runoff = wetness * (SOIL_STEPS * surface.reshape(rows, lanes) + (base_drain + source * unit_drain))
    return (moisture.reshape(layers, rows * lanes), runoff.reshape(rows * lanes))


CAP_P = 4
CAP_R = 2


def id_rows(ids, width):
    flat = ids.reshape(-1)
    return jnp.pad(flat, (0, 8 * width - flat.shape[0])).reshape(8, width)


def route_partials(partial_value, pair_land, tile_count, sub_count, tile_index):
    pair_count, field_count, width = partial_value.shape
    owner_device = pair_land // LB_DEV
    tile_step = (owner_device // sub_count - tile_index + 1 + tile_count) % tile_count
    dest_sub = owner_device % sub_count
    group_count = 3 * sub_count
    group_id = dest_sub * 3 + tile_step
    hits = (group_id[:, None] == jnp.arange(group_count, dtype=jnp.int32)[None, :]).astype(jnp.int32)
    ranks = jnp.sum((jnp.cumsum(hits, axis=0) - hits) * hits, axis=1)
    slot_id = group_id * CAP_P + ranks
    slot_count = group_count * CAP_P
    placing = slot_id[None, :] == jnp.arange(slot_count, dtype=jnp.int32)[:, None]
    source = jnp.sum(jnp.where(placing, jnp.arange(pair_count, dtype=jnp.int32)[None, :] + 1, 0), axis=1) - 1
    filled = source >= 0
    picked = jnp.maximum(source, 0)
    rows = jnp.where(filled[:, None, None], partial_value[picked], 0.0)
    ids = jnp.where(filled, pair_land[picked] % LB_DEV, -1).astype(jnp.float32)
    chunk_rows = 3 * CAP_P * field_count
    ids = ids.reshape(sub_count, 3 * CAP_P)
    chunks = jnp.concatenate(
        [
            rows.reshape(sub_count, chunk_rows, width),
            jnp.stack([id_rows(ids[j], width) for j in range(sub_count)]),
        ],
        axis=1,
    )
    by_sub = lax.all_to_all(chunks, "sub", split_axis=0, concat_axis=0, tiled=True)
    part_rows = CAP_P * field_count
    got_ids = by_sub[:, chunk_rows, : 3 * CAP_P]
    messages = []
    for tile_step in range(3):
        data = by_sub[:, tile_step * part_rows : (tile_step + 1) * part_rows, :]
        data = data.reshape(sub_count * part_rows, width)
        step_ids = got_ids[:, tile_step * CAP_P : (tile_step + 1) * CAP_P]
        messages.append(jnp.concatenate([data, id_rows(step_ids, width)], axis=0))
    devices = range(tile_count)
    received = [
        lax.ppermute(messages[0], "tile", [(i, (i - 1) % tile_count) for i in devices]),
        messages[1],
        lax.ppermute(messages[2], "tile", [(i, (i + 1) % tile_count) for i in devices]),
    ]
    message_rows = sub_count * part_rows
    data = jnp.concatenate([m[:message_rows] for m in received], axis=0)
    slot_ids = jnp.concatenate([m[message_rows, : sub_count * CAP_P] for m in received])
    selector = (slot_ids[None, :] == jnp.arange(LB_DEV, dtype=jnp.float32)[:, None]).astype(jnp.float32)
    data = data.reshape(slot_ids.shape[0], field_count, width)
    return jnp.einsum("bs,sfl->fbl", selector, data, precision=lax.Precision.HIGHEST)


def on_device(
    atm_fields, pair_atm, pair_land, pair_weight, land_mask, conductance, soil_moisture, river_owner
):
    tile_count = lax.axis_size("tile")
    sub_count = lax.axis_size("sub")
    tile_index = lax.axis_index("tile")
    sub_index = lax.axis_index("sub")
    field_count, row_count, row_width = atm_fields.shape
    pair_count = pair_atm.shape[0]
    owners = river_owner.shape[0]
    small = lax.optimization_barrier(jnp.concatenate([pair_atm, pair_land, river_owner]))
    pair_atm = small[:pair_count]
    pair_land = small[pair_count : 2 * pair_count]
    river_owner = small[2 * pair_count : 2 * pair_count + owners]
    devices = tile_count * sub_count
    up = [(i, (i + 1) % devices) for i in range(devices)]
    down = [(j, i) for i, j in up]
    before = lax.ppermute(atm_fields[:, row_count - 1 :, :], ("tile", "sub"), up)
    local_rows = lax.optimization_barrier(jnp.pad(atm_fields, ((0, 0), (0, 0), (0, row_width))))
    atm_fields = local_rows[:, :, :row_width]
    after = lax.ppermute(atm_fields[:, :1, :], ("tile", "sub"), down)
    extended = jnp.concatenate([before, atm_fields, after], axis=1)
    grad_x = x_gradient(atm_fields)
    grad_y = (extended[:, 2:, :] - extended[:, :-2, :]) * 0.5
    plain = jnp.concatenate([atm_fields, grad_x], axis=2).astype(jnp.bfloat16)
    weights = pair_weight.reshape(pair_count, 3 * row_width, LBLK)
    partial_value = jnp.einsum(
        "fpk,pkl->pfl",
        plain[:, pair_atm, :],
        weights[:, : 2 * row_width, :],
        preferred_element_type=jnp.float32,
    ) + jnp.einsum(
        "fpk,pkl->pfl",
        grad_y.astype(jnp.bfloat16)[:, pair_atm, :],
        weights[:, 2 * row_width :, :],
        preferred_element_type=jnp.float32,
    )
    owned_sums = route_partials(partial_value, pair_land, tile_count, sub_count, tile_index)
    forcing = owned_sums.reshape(field_count, LB_DEV * LBLK)
    land_forcing = forcing.astype(jnp.bfloat16)
    layers, cell_count = conductance.shape
    tiles = (cell_count // RBLK, RBLK)
    response = soil_response(
        conductance.reshape((layers,) + tiles), soil_moisture.reshape((layers,) + tiles)
    )
    wetness = land_mask.astype(jnp.float32)
    source = wetness * (
        jax.nn.softplus(forcing[0]) * jax.nn.sigmoid(forcing[1])
        - 0.5 * jax.nn.sigmoid(forcing[2]) * jax.nn.softplus(forcing[3])
    )
    surface = wetness * jax.nn.softplus(forcing[0]) * (1.0 - jax.nn.sigmoid(forcing[1]))
    moisture, runoff = soil_update(source, surface, wetness.reshape(tiles), response)
    block_count = runoff.shape[0] // RBLK
    capacity = CAP_R
    runoff_blocks = runoff.reshape(block_count, RBLK)
    hits = (river_owner[:, None] == jnp.arange(tile_count, dtype=jnp.int32)[None, :]).astype(
        jnp.int32
    )
    ranks = jnp.sum((jnp.cumsum(hits, axis=0) - hits) * hits, axis=1)
    slot_id = river_owner * capacity + ranks
    placing = slot_id[None, :] == jnp.arange(tile_count * capacity, dtype=jnp.int32)[:, None]
    values = jnp.dot(placing.astype(jnp.float32), runoff_blocks, precision=lax.Precision.HIGHEST)
    values = values.reshape(tile_count, capacity * RBLK)
    block_ids = (tile_index * sub_count + sub_index) * block_count + jnp.arange(
        block_count, dtype=jnp.int32
    )
    numbers = jnp.sum(jnp.where(placing, block_ids[None, :] + 1, 0), axis=1) - 1
    numbers = numbers.astype(jnp.float32).reshape(tile_count, capacity)
    numbers = jnp.pad(numbers, ((0, 0), (0, RBLK - capacity)))
    packed = jnp.concatenate([values, numbers], axis=1)
    got = lax.all_to_all(packed, "tile", split_axis=0, concat_axis=0, tiled=True)
    river_runoff = got[:, : capacity * RBLK].reshape(tile_count, capacity, RBLK)[None, None]
    river_blocks = got[:, capacity * RBLK : capacity * RBLK + capacity].astype(jnp.int32)[None, None]
    return (land_forcing, moisture, river_runoff, river_blocks)


def solution(mesh):
    return jax.shard_map(
        on_device,
        mesh=mesh,
        in_specs=(
            P(None, ("tile", "sub"), None),
            P(("tile", "sub")),
            P(("tile", "sub")),
            P(("tile", "sub"), None, None, None),
            P(("tile", "sub")),
            P(None, ("tile", "sub")),
            P(None, ("tile", "sub")),
            P(("tile", "sub")),
        ),
        out_specs=(
            P(None, ("tile", "sub")),
            P(None, ("tile", "sub")),
            P("tile", "sub", None, None, None),
            P("tile", "sub", None, None),
        ),
        check_vma=False,
    )
```

```python
import jax
import jax.numpy as jnp
from jax import lax
from jax.sharding import PartitionSpec as P
from jax.experimental import pallas as pl
from jax.experimental.pallas import tpu as pltpu

SOIL_STEPS = 4
LBLK = 512
RBLK = 128
LB_DEV = 16


def passed_along(block, axis, distance):
    devices = range(lax.axis_size(axis))
    route = [((i - distance) % len(devices), i) for i in devices]
    return lax.ppermute(block, axis, route)


def padded(array, sides, width):
    for axis, dim in sides:
        devices, length = (lax.axis_size(axis), array.shape[dim])
        up = [(i, (i + 1) % devices) for i in range(devices)]
        down = [(j, i) for i, j in up]
        last = lax.slice_in_dim(array, length - width, length, axis=dim)
        initial = lax.slice_in_dim(array, 0, width, axis=dim)
        before = lax.ppermute(last, axis, up)
        after = lax.ppermute(initial, axis, down)
        array = jnp.concatenate([before, array, after], axis=dim)
    return array


def x_gradient(fields):
    inner = (fields[:, :, 2:] - fields[:, :, :-2]) * 0.5
    first = fields[:, :, 1:2] - fields[:, :, 0:1]
    last = fields[:, :, -1:] - fields[:, :, -2:-1]
    return jnp.concatenate([first, inner, last], axis=2)


def column_factors(conductance):
    layers = conductance.shape[0]
    inverse = []
    ratios = []
    for k in range(layers):
        diagonal = 1.0 + conductance[k]
        if k > 0:
            diagonal = (
                diagonal
                + conductance[k - 1]
                - conductance[k - 1] * conductance[k - 1] * inverse[k - 1]
            )
        pivot_inv = 1.0 / diagonal
        inverse.append(pivot_inv)
        ratios.append(-conductance[k] * pivot_inv)
    return (inverse, ratios)


def column_solve(moisture, source, conductance, inverse, ratios):
    layers = len(inverse)
    forward = []
    for k in range(layers):
        if k == 0:
            column_value = moisture[0] + source
        else:
            column_value = moisture[k] + conductance[k - 1] * forward[k - 1]
        forward.append(column_value * inverse[k])
    solved = [forward[layers - 1]]
    for k in range(layers - 2, -1, -1):
        solved.insert(0, forward[k] - ratios[k] * solved[0])
    return jnp.stack(solved)


def response_kernel(
    cond_ref, moist_ref, base_ref, unit_ref, base_drain_ref, unit_drain_ref, inv_ref, ratio_ref
):
    layers = cond_ref.shape[0]
    rows = pl.ds(0, cond_ref.shape[1])
    previous_cond = None
    previous_inv = None
    for k in range(layers):
        cond = cond_ref[k, rows, :]
        diagonal = 1.0 + cond
        if k > 0:
            diagonal = diagonal + previous_cond - previous_cond * previous_cond * previous_inv
        pivot_inv = 1.0 / diagonal
        inv_ref[k] = pivot_inv
        ratio_ref[k] = -cond * pivot_inv
        previous_cond = cond
        previous_inv = pivot_inv

    def solve(moisture, source):
        drainage = None
        for substep in range(SOIL_STEPS):
            forward = []
            for k in range(layers):
                if k == 0:
                    column_value = moisture[0] if source is None else moisture[0] + source
                else:
                    column_value = moisture[k] + cond_ref[k - 1, rows, :] * forward[k - 1]
                forward.append(column_value * inv_ref[k])
            solved = [forward[layers - 1]]
            for k in range(layers - 2, -1, -1):
                solved.insert(0, forward[k] - ratio_ref[k] * solved[0])
            moisture = solved
            drained = cond_ref[layers - 1, rows, :] * moisture[layers - 1]
            drainage = drained if drainage is None else drainage + drained
        return (moisture, drainage)

    base, base_drain = solve([moist_ref[k, rows, :] for k in range(layers)], None)
    for k in range(layers):
        base_ref[k, rows, :] = base[k]
    base_drain_ref[rows, :] = base_drain
    zero = jnp.zeros_like(base_drain)
    unit, unit_drain = solve([zero] * layers, zero + 1.0)
    for k in range(layers):
        unit_ref[k, rows, :] = unit[k]
    unit_drain_ref[rows, :] = unit_drain


def soil_response(conductance, soil_moisture):
    layers, rows, lanes = conductance.shape
    grid = 2
    block = rows // grid
    plane = pl.BlockSpec((block, lanes), lambda i: (i, 0))
    stack = pl.BlockSpec((layers, block, lanes), lambda i: (0, i, 0))
    layer_shape = jax.ShapeDtypeStruct((layers, rows, lanes), jnp.float32)
    plane_shape = jax.ShapeDtypeStruct((rows, lanes), jnp.float32)
    return pl.pallas_call(
        response_kernel,
        grid=(grid,),
        in_specs=[stack, stack],
        out_specs=[stack, stack, plane, plane],
        scratch_shapes=[pltpu.VMEM((layers, block, lanes), jnp.float32)] * 2,
        out_shape=[layer_shape, layer_shape, plane_shape, plane_shape],
    )(conductance, soil_moisture)


def soil_update(source, surface, wetness, response):
    base, unit, base_drain, unit_drain = response
    layers, rows, lanes = base.shape
    source = source.reshape(rows, lanes)
    moisture = base + source[None] * unit
    runoff = wetness * (SOIL_STEPS * surface.reshape(rows, lanes) + (base_drain + source * unit_drain))
    return (moisture.reshape(layers, rows * lanes), runoff.reshape(rows * lanes))


CAP_P = 4
CAP_R = 2


def id_rows(ids, width):
    flat = ids.reshape(-1)
    return jnp.pad(flat, (0, 8 * width - flat.shape[0])).reshape(8, width)


def route_partials(partial_value, pair_land, tile_count, sub_count, tile_index):
    pair_count, field_count, width = partial_value.shape
    owner_device = pair_land // LB_DEV
    tile_step = (owner_device // sub_count - tile_index + 1 + tile_count) % tile_count
    dest_sub = owner_device % sub_count
    group_count = 3 * sub_count
    group_id = dest_sub * 3 + tile_step
    hits = (group_id[:, None] == jnp.arange(group_count, dtype=jnp.int32)[None, :]).astype(jnp.int32)
    ranks = jnp.sum((jnp.cumsum(hits, axis=0) - hits) * hits, axis=1)
    slot_id = group_id * CAP_P + ranks
    slot_count = group_count * CAP_P
    placing = slot_id[None, :] == jnp.arange(slot_count, dtype=jnp.int32)[:, None]
    source = jnp.sum(jnp.where(placing, jnp.arange(pair_count, dtype=jnp.int32)[None, :] + 1, 0), axis=1) - 1
    filled = source >= 0
    picked = jnp.maximum(source, 0)
    choose = (source[:, None] == jnp.arange(pair_count, dtype=jnp.int32)[None, :]).astype(jnp.float32)
    rows = jnp.dot(
        choose, partial_value.reshape(pair_count, field_count * width), precision=lax.Precision.HIGHEST
    ).reshape(source.shape[0], field_count, width)
    ids = jnp.where(filled, pair_land[picked] % LB_DEV, -1).astype(jnp.float32)
    chunk_rows = 3 * CAP_P * field_count
    ids = ids.reshape(sub_count, 3 * CAP_P)
    chunks = jnp.concatenate(
        [
            rows.reshape(sub_count, chunk_rows, width),
            jnp.stack([id_rows(ids[j], width) for j in range(sub_count)]),
        ],
        axis=1,
    )
    by_sub = lax.all_to_all(chunks, "sub", split_axis=0, concat_axis=0, tiled=True)
    part_rows = CAP_P * field_count
    got_ids = by_sub[:, chunk_rows, : 3 * CAP_P]
    messages = []
    for tile_step in range(3):
        data = by_sub[:, tile_step * part_rows : (tile_step + 1) * part_rows, :]
        data = data.reshape(sub_count * part_rows, width)
        step_ids = got_ids[:, tile_step * CAP_P : (tile_step + 1) * CAP_P]
        messages.append(jnp.concatenate([data, id_rows(step_ids, width)], axis=0))
    devices = range(tile_count)
    received = [
        lax.ppermute(messages[0], "tile", [(i, (i - 1) % tile_count) for i in devices]),
        messages[1],
        lax.ppermute(messages[2], "tile", [(i, (i + 1) % tile_count) for i in devices]),
    ]
    message_rows = sub_count * part_rows
    data = jnp.concatenate([m[:message_rows] for m in received], axis=0)
    slot_ids = jnp.concatenate([m[message_rows, : sub_count * CAP_P] for m in received])
    selector = (slot_ids[None, :] == jnp.arange(LB_DEV, dtype=jnp.float32)[:, None]).astype(jnp.float32)
    data = data.reshape(slot_ids.shape[0], field_count, width)
    return jnp.einsum("bs,sfl->fbl", selector, data, precision=lax.Precision.HIGHEST)


def on_device(
    atm_fields, pair_atm, pair_land, pair_weight, land_mask, conductance, soil_moisture, river_owner
):
    tile_count = lax.axis_size("tile")
    sub_count = lax.axis_size("sub")
    tile_index = lax.axis_index("tile")
    sub_index = lax.axis_index("sub")
    field_count, row_count, row_width = atm_fields.shape
    pair_count = pair_atm.shape[0]
    owners = river_owner.shape[0]
    small = lax.optimization_barrier(jnp.concatenate([pair_atm, pair_land, river_owner]))
    pair_atm = small[:pair_count]
    pair_land = small[pair_count : 2 * pair_count]
    river_owner = small[2 * pair_count : 2 * pair_count + owners]
    devices = tile_count * sub_count
    up = [(i, (i + 1) % devices) for i in range(devices)]
    down = [(j, i) for i, j in up]
    before = lax.ppermute(atm_fields[:, row_count - 1 :, :], ("tile", "sub"), up)
    local_rows = lax.optimization_barrier(jnp.pad(atm_fields, ((0, 0), (0, 0), (0, row_width))))
    atm_fields = local_rows[:, :, :row_width]
    after = lax.ppermute(atm_fields[:, :1, :], ("tile", "sub"), down)
    extended = jnp.concatenate([before, atm_fields, after], axis=1)
    grad_x = x_gradient(atm_fields)
    grad_y = (extended[:, 2:, :] - extended[:, :-2, :]) * 0.5
    stacked = jnp.concatenate([atm_fields, grad_x, grad_y], axis=2).astype(jnp.bfloat16)
    picked = stacked[:, pair_atm, :]
    weights = pair_weight.reshape(pair_count, 3 * row_width, LBLK)
    partial_value = jnp.einsum("fpk,pkl->pfl", picked, weights, preferred_element_type=jnp.float32)
    owned_sums = route_partials(partial_value, pair_land, tile_count, sub_count, tile_index)
    forcing = owned_sums.reshape(field_count, LB_DEV * LBLK)
    land_forcing = forcing.astype(jnp.bfloat16)
    layers, cell_count = conductance.shape
    tiles = (cell_count // RBLK, RBLK)
    response = soil_response(
        conductance.reshape((layers,) + tiles), soil_moisture.reshape((layers,) + tiles)
    )
    wetness = land_mask.astype(jnp.float32)
    source = wetness * (
        jax.nn.softplus(forcing[0]) * jax.nn.sigmoid(forcing[1])
        - 0.5 * jax.nn.sigmoid(forcing[2]) * jax.nn.softplus(forcing[3])
    )
    surface = wetness * jax.nn.softplus(forcing[0]) * (1.0 - jax.nn.sigmoid(forcing[1]))
    moisture, runoff = soil_update(source, surface, wetness.reshape(tiles), response)
    block_count = runoff.shape[0] // RBLK
    capacity = CAP_R
    runoff_blocks = runoff.reshape(block_count, RBLK)
    hits = (river_owner[:, None] == jnp.arange(tile_count, dtype=jnp.int32)[None, :]).astype(
        jnp.int32
    )
    ranks = jnp.sum((jnp.cumsum(hits, axis=0) - hits) * hits, axis=1)
    slot_id = river_owner * capacity + ranks
    placing = slot_id[None, :] == jnp.arange(tile_count * capacity, dtype=jnp.int32)[:, None]
    values = jnp.dot(placing.astype(jnp.float32), runoff_blocks, precision=lax.Precision.HIGHEST)
    values = values.reshape(tile_count, capacity * RBLK)
    block_ids = (tile_index * sub_count + sub_index) * block_count + jnp.arange(
        block_count, dtype=jnp.int32
    )
    numbers = jnp.sum(jnp.where(placing, block_ids[None, :] + 1, 0), axis=1) - 1
    numbers = numbers.astype(jnp.float32).reshape(tile_count, capacity)
    numbers = jnp.pad(numbers, ((0, 0), (0, RBLK - capacity)))
    packed = jnp.concatenate([values, numbers], axis=1)
    got = lax.all_to_all(packed, "tile", split_axis=0, concat_axis=0, tiled=True)
    river_runoff = got[:, : capacity * RBLK].reshape(tile_count, capacity, RBLK)[None, None]
    river_blocks = got[:, capacity * RBLK : capacity * RBLK + capacity].astype(jnp.int32)[None, None]
    return (land_forcing, moisture, river_runoff, river_blocks)


def solution(mesh):
    return jax.shard_map(
        on_device,
        mesh=mesh,
        in_specs=(
            P(None, ("tile", "sub"), None),
            P(("tile", "sub")),
            P(("tile", "sub")),
            P(("tile", "sub"), None, None, None),
            P(("tile", "sub")),
            P(None, ("tile", "sub")),
            P(None, ("tile", "sub")),
            P(("tile", "sub")),
        ),
        out_specs=(
            P(None, ("tile", "sub")),
            P(None, ("tile", "sub")),
            P("tile", "sub", None, None, None),
            P("tile", "sub", None, None),
        ),
        check_vma=False,
    )
```
